128 devices in a mesh: batch: 16 (over z_lo, x, core), patch: 8 (over z_hi, y).
Axes of the slice: x: 4, y: 4, z: 4 (z_hi: 2, z_lo: 2; z = z_hi * 2 + z_lo), core: 2. Of those that a mesh axis runs over, the one named last changes fastest.
Arguments:
- hidden_in: bfloat16 [49152, 1280], P(('batch', 'patch')), parts along dimension 0, may hold values from -45 to 45
- stale_keys: bfloat16 [49152, 1280], P(('batch', 'patch')), parts along dimension 0, may hold values from -150 to 150
- stale_values: bfloat16 [49152, 1280], P(('batch', 'patch')), parts along dimension 0, may hold values from -12 to 12
- stale_moments: float32 [768, 2, 2, 32], P(('batch', 'patch')), parts along dimension 0, may hold values from -5120 to 102400, as said below
- gain_attn: float32 [1280], replicated, may hold values from 0.1 to 1.9
- bias_attn: float32 [1280], replicated, may hold values from -3 to 3
- w_query: bfloat16 [1280, 1280], replicated, may hold values from -0.3125 to 0.3125
- w_key: bfloat16 [1280, 1280], replicated, may hold values from -0.625 to 0.625
- w_value: bfloat16 [1280, 1280], replicated, may hold values from -0.625 to 0.625
- gain_conv: float32 [1280], replicated, may hold values from 0.1 to 1.9
- bias_conv: float32 [1280], replicated, may hold values from -3 to 3
- conv_weight: bfloat16 [3, 3, 1280, 640], replicated, may hold values from -0.0546875 to 0.0546875
- conv_bias: float32 [640], replicated, may hold values from -3 to 3
- w_time: bfloat16 [320, 640], replicated, may hold values from -0.3125 to 0.3125
- timestep: int32 [1], replicated, may hold values from 0 to 999
Outputs:
- conv_out: bfloat16 [49152, 640], P(('batch', 'patch')), parts along dimension 0
The draws below stay inside these ranges and needn't reach their ends.
There are 16 independent parts, one for each index of `batch`. The reference program is written for one: setup_inputs(seed, part) draws one part's arguments, and reference() takes and returns one part's arrays. A program takes and returns all parts, laid end to end along the dimension named above; an argument that names none is the same for every part. Nothing has to cross between parts.
Inputs may be any that keep to these rules, and one draw needn't show every extreme that they name: `stale_moments`: each row's entries are the sums and sums of squares of 2560 values: that count times the second is at least the square of the first.
All inputs are finite; a program needn't handle non-finite values.
Results may differ from the reference program's by a relative error of at most 0.008.
The reference program's roundings to bfloat16 on the way count: a program that leaves them out, or rounds other values in their place, can miss the bound.
Values may be sent and summed in bfloat16 or wider, within the bound.
No kernel may reach another device: no remote copies, remote signals or barrier semaphores. Data moves between devices by JAX's collectives and lax.ppermute only.
A program may use at most 320 MiB of HBM per device.

```python
import math
import jax
import jax.numpy as jnp
from jax import lax

HEADS = 20
HEAD_DIM = 64
GROUPS = 32
TDIM = 320
COUT = 640
W = 64
ROWS_DEV = 6
C = 1280
TOK_DEV = 384
NROWS = 48
NTOK = 3072
N_PATCH = 8


def draw_hidden_in(key, part):
    key_one, key_two, key_three = jax.random.split(key, 3)
    row_scale = jnp.exp(jax.random.uniform(key_two, (NTOK, 1), minval=math.log(0.5), maxval=math.log(3.0)))
    chan_scale = jnp.exp(jax.random.uniform(key_three, (1, C), minval=math.log(0.5), maxval=math.log(3.0)))
    sampled = jnp.clip(jax.random.normal(key_one, (NTOK, C)), -5.0, 5.0) * row_scale
    return (sampled * chan_scale).astype(jnp.bfloat16)


def stale_pair(key):
    base_key = jax.random.fold_in(key, 17)
    key_one = jax.random.fold_in(base_key, 0)
    key_four = jax.random.fold_in(base_key, 3)
    sampled = 4.0 * jnp.clip(jax.random.normal(key_one, (NTOK, C)), -5.0, 5.0)
    noise = jnp.clip(jax.random.normal(key_four, (NTOK, C)), -5.0, 5.0)
    keys_drawn = sampled.astype(jnp.bfloat16)
    values_drawn = jnp.clip(0.5 * sampled + noise, -12.0, 12.0).astype(jnp.bfloat16)
    return (keys_drawn, values_drawn)


def draw_stale_keys(key, part):
    return stale_pair(key)[0]


def draw_stale_values(key, part):
    return stale_pair(key)[1]


def draw_stale_moments(key, part):
    key_one, key_two = jax.random.split(key, 2)
    cells = W * (C // GROUPS)
    positions = jnp.arange(NROWS, dtype=jnp.float32) / max(NROWS - 1, 1)
    rising = (10.0 ** positions)[:, None, None]
    variance = rising * jnp.exp(jax.random.uniform(key_one, (NROWS, 2, GROUPS), minval=math.log(0.5), maxval=math.log(2.0)))
    average = jnp.clip(jax.random.normal(key_two, (NROWS, 2, GROUPS)), -2.0, 2.0)
    first_sum = cells * average
    second_sum = cells * (variance + average * average)
    return jnp.stack([first_sum, second_sum], axis=2).astype(jnp.float32)


def bell_draw(rng, extent, width, bound, held_as=jnp.bfloat16):
    return jnp.clip(width * jax.random.normal(rng, extent, jnp.float32), -bound, bound).astype(held_as)


def setup_inputs(seed: int = 0, part: int = 0) -> dict:
    key_list = jax.random.split(jax.random.key(seed), 16)
    own_keys = jax.random.split(jax.random.fold_in(key_list[15], part), 16)
    return {
        "hidden_in": draw_hidden_in(jax.random.fold_in(jax.random.fold_in(key_list[15], part), 71), part),
        "stale_keys": draw_stale_keys(jax.random.fold_in(jax.random.fold_in(key_list[15], part), 71), part),
        "stale_values": draw_stale_values(jax.random.fold_in(jax.random.fold_in(key_list[15], part), 71), part),
        "stale_moments": draw_stale_moments(jax.random.fold_in(jax.random.fold_in(key_list[15], part), 71), part),
        "gain_attn": jnp.clip(1.0 + 0.18 * jax.random.normal(key_list[4], (C,), jnp.float32), 0.1, 1.9),
        "bias_attn": bell_draw(key_list[5], (C,), 0.5, 3.0, jnp.float32),
        "w_query": bell_draw(key_list[6], (C, C), (C // 4) ** -0.5, 0.3125),
        "w_key": bell_draw(key_list[7], (C, C), (C // 16) ** -0.5, 0.625),
        "w_value": bell_draw(key_list[8], (C, C), (C // 16) ** -0.5, 0.625),
        "gain_conv": jnp.clip(1.0 + 0.18 * jax.random.normal(key_list[9], (C,), jnp.float32), 0.1, 1.9),
        "bias_conv": bell_draw(key_list[10], (C,), 0.5, 3.0, jnp.float32),
        "conv_weight": bell_draw(key_list[11], (3, 3, C, COUT), (9 * C) ** -0.5, 0.0546875),
        "conv_bias": bell_draw(key_list[12], (COUT,), 0.5, 3.0, jnp.float32),
        "w_time": bell_draw(key_list[13], (TDIM, COUT), TDIM ** -0.5, 0.3125),
        "timestep": jax.random.randint(key_list[14], (1,), 0, 1000).astype(jnp.int32),
    }


EPS = 1e-05

def group_moments(rows_in, groups):
    values = rows_in.astype(jnp.float32).reshape(rows_in.shape[0], groups, rows_in.shape[1] // groups)
    return jnp.stack([lax.optimization_barrier(jnp.sum(values, axis=(0, 2))), lax.optimization_barrier(jnp.sum(values * values, axis=(0, 2)))])

def group_normalize(rows_in, totals, count, gain, offset, groups):
    average = totals[0] / count
    variance = totals[1] / count - average * average
    inverse = lax.rsqrt(variance + EPS)
    group_width = rows_in.shape[1] // groups
    factors = jnp.repeat(inverse, group_width) * gain
    shifts = offset - jnp.repeat(average * inverse, group_width) * gain
    return rows_in.astype(jnp.float32) * factors + shifts

def time_embedding(timestep, w_time):
    half_dim = w_time.shape[0] // 2
    frequency = jnp.exp(-math.log(10000.0) * jnp.arange(half_dim, dtype=jnp.float32) / half_dim)
    angles = timestep[0].astype(jnp.float32) * frequency
    embedded = jnp.concatenate([jnp.cos(angles), jnp.sin(angles)])
    return jnp.dot(embedded[None, :], w_time.astype(jnp.float32), precision=lax.Precision.HIGHEST)[0]

def reference(hidden_in, stale_keys, stale_values, stale_moments, gain_attn, bias_attn, w_query, w_key, w_value, gain_conv, bias_conv, conv_weight, conv_bias, w_time, timestep):
    count = NTOK * (C // GROUPS)
    stale_total = lax.optimization_barrier(jnp.sum(stale_moments, axis=0))
    scale_qk = HEAD_DIM ** (-0.5)

    def strip_result(strip):
        first_tok = (strip * TOK_DEV).astype(jnp.int32)
        first_row = (strip * ROWS_DEV).astype(jnp.int32)
        rows_in = lax.dynamic_slice_in_dim(hidden_in, first_tok, TOK_DEV, 0)
        stale_strip = lax.optimization_barrier(jnp.sum(lax.dynamic_slice_in_dim(stale_moments, first_row, ROWS_DEV, 0), axis=0))
        totals_attn = stale_total[0] - stale_strip[0] + group_moments(rows_in, GROUPS)
        normed = group_normalize(rows_in, totals_attn, count, gain_attn, bias_attn, GROUPS).astype(jnp.bfloat16)
        query = jnp.dot(normed, w_query, preferred_element_type=jnp.float32).astype(jnp.bfloat16)
        key_fresh = jnp.dot(normed, w_key, preferred_element_type=jnp.float32).astype(jnp.bfloat16)
        value_fresh = jnp.dot(normed, w_value, preferred_element_type=jnp.float32).astype(jnp.bfloat16)
        keys_used = lax.dynamic_update_slice_in_dim(stale_keys, key_fresh, first_tok, 0)
        values_used = lax.dynamic_update_slice_in_dim(stale_values, value_fresh, first_tok, 0)
        query3 = query.astype(jnp.float32).reshape(TOK_DEV, HEADS, HEAD_DIM)
        keys3 = keys_used.astype(jnp.float32).reshape(NTOK, HEADS, HEAD_DIM)
        values3 = values_used.astype(jnp.float32).reshape(NTOK, HEADS, HEAD_DIM)
        scores = jnp.einsum('qhd,khd->qhk', query3, keys3) * scale_qk
        row_max = lax.optimization_barrier(jnp.max(scores, axis=-1, keepdims=True))
        weights = jnp.exp(scores - row_max)
        row_total = lax.optimization_barrier(jnp.sum(weights, axis=-1))
        probs = weights.astype(jnp.bfloat16).astype(jnp.float32)
        weighted = jnp.einsum('qhk,khd->qhd', probs, values3)
        attended = (weighted / row_total[..., None]).reshape(TOK_DEV, C)
        updated = (rows_in.astype(jnp.float32) + attended).astype(jnp.bfloat16)
        totals_conv = stale_total[1] - stale_strip[1] + group_moments(updated, GROUPS)
        normed_conv = group_normalize(updated, totals_conv, count, gain_conv, bias_conv, GROUPS)
        return jax.nn.silu(normed_conv).astype(jnp.bfloat16)
    strips = lax.map(strip_result, jnp.arange(N_PATCH, dtype=jnp.int32))
    latent_grid = strips.reshape(1, NROWS, W, C)
    convolved = lax.conv_general_dilated(latent_grid, conv_weight, (1, 1), ((1, 1), (1, 1)), dimension_numbers=('NHWC', 'HWIO', 'NHWC'), preferred_element_type=jnp.float32)[0]
    temb = time_embedding(timestep, w_time)
    conv_out = (convolved + conv_bias + temb).astype(jnp.bfloat16)
    return conv_out.reshape(NTOK, COUT)
```

```python
import math

import jax
import jax.numpy as jnp
from jax import lax
from jax.sharding import PartitionSpec as P
from jax.experimental import pallas as pl
from jax.experimental.pallas import tpu as pltpu

HEADS = 20
GROUPS = 32
W = 64
NCHUNK = 2
QBLK = 128


EPS = 1e-05
NEG = -1e30


def padded_2(cells, sides, width):
    for axis, dim in sides:
        count = lax.axis_size(axis)
        ends = count - 1
        head = lax.slice_in_dim(cells, 0, width, axis=dim)
        tail = lax.slice_in_dim(cells, cells.shape[dim] - width, cells.shape[dim], axis=dim)
        cells = jnp.concatenate(
            [
                lax.ppermute(tail, axis, [(i, (i + 1) % count) for i in range(ends)]),
                cells,
                lax.ppermute(head, axis, [((i + 1) % count, i) for i in range(ends)]),
            ],
            axis=dim,
        )
    return cells


def group_moments(rows_in, groups):
    values = rows_in.astype(jnp.float32).reshape(
        rows_in.shape[0], groups, rows_in.shape[1] // groups
    )
    return jnp.stack([jnp.sum(values, axis=(0, 2)), jnp.sum(values * values, axis=(0, 2))])


def group_normalize(rows_in, totals, count, gain, offset, groups):
    average = totals[0] / count
    variance = totals[1] / count - average * average
    inverse = lax.rsqrt(variance + EPS)
    group_width = rows_in.shape[1] // groups
    factors = jnp.repeat(inverse, group_width) * gain
    shifts = offset - jnp.repeat(average * inverse, group_width) * gain
    return rows_in.astype(jnp.float32) * factors + shifts


def time_embedding(timestep, w_time):
    half_dim = w_time.shape[0] // 2
    frequency = jnp.exp(-math.log(10000.0) * jnp.arange(half_dim, dtype=jnp.float32) / half_dim)
    angles = timestep[0].astype(jnp.float32) * frequency
    embedded = jnp.concatenate([jnp.cos(angles), jnp.sin(angles)])
    return jnp.dot(embedded[None, :], w_time.astype(jnp.float32), precision=lax.Precision.HIGHEST)[
        0
    ]


def attn_kernel(q_ref, k_ref, v_ref, h_ref, o_ref):
    head_dim = q_ref.shape[1] // 2
    scale = head_dim ** (-0.5)
    for hh in range(2):
        lanes = slice(hh * head_dim, (hh + 1) * head_dim)
        kh = k_ref[:, lanes]
        vh = v_ref[:, lanes]
        for qb in range(q_ref.shape[0] // QBLK):
            rows = slice(qb * QBLK, (qb + 1) * QBLK)
            qh = q_ref[rows, lanes]
            s = lax.dot_general(
                qh, kh, (((1,), (1,)), ((), ())), preferred_element_type=jnp.float32
            ) * scale
            m = jnp.max(s, axis=1, keepdims=True)
            w = jnp.exp(s - m)
            total = jnp.sum(w, axis=1, keepdims=True)
            acc = jnp.dot(w.astype(jnp.bfloat16), vh, preferred_element_type=jnp.float32)
            att = acc / total
            o_ref[rows, lanes] = (h_ref[rows, lanes].astype(jnp.float32) + att).astype(
                jnp.bfloat16
            )


def attention_chunk(query, keys, values, hidden, chunk):
    tok_rows, width = query.shape
    key_count = keys.shape[0]
    pairs = width // 128
    return pl.pallas_call(
        attn_kernel,
        grid=(pairs,),
        in_specs=[
            pl.BlockSpec((tok_rows, 128), lambda h: (0, h)),
            pl.BlockSpec((key_count, 128), lambda h: (0, h)),
            pl.BlockSpec((key_count, 128), lambda h: (0, h)),
            pl.BlockSpec((tok_rows, 128), lambda h: (0, h + chunk * pairs)),
        ],
        out_specs=pl.BlockSpec((tok_rows, 128), lambda h: (0, h)),
        out_shape=jax.ShapeDtypeStruct((tok_rows, width), jnp.bfloat16),
        compiler_params=pltpu.CompilerParams(vmem_limit_bytes=48 * 1024 * 1024),
    )(query, keys, values, hidden)


def body(
    hidden_in,
    stale_keys,
    stale_values,
    stale_moments,
    gain_attn,
    bias_attn,
    w_query,
    w_key,
    w_value,
    gain_conv,
    bias_conv,
    conv_weight,
    conv_bias,
    w_time,
    timestep,
):
    devices = lax.axis_size("patch")
    position = lax.axis_index("patch")
    tok_rows = hidden_in.shape[0]
    channels = hidden_in.shape[1]
    all_tokens = tok_rows * devices
    count = all_tokens * (channels // GROUPS)
    own_first = position * tok_rows
    width = channels // NCHUNK
    gathered = []
    for c in range(NCHUNK):
        cols = slice(c * width, (c + 1) * width)
        gathered.append(
            (
                lax.all_gather(stale_keys[:, cols], "patch", axis=0, tiled=True),
                lax.all_gather(stale_values[:, cols], "patch", axis=0, tiled=True),
            )
        )
    own_stale = jnp.sum(stale_moments, axis=0)
    total_attn = lax.psum(own_stale[0], "patch")
    totals_attn = total_attn - own_stale[0] + group_moments(hidden_in, GROUPS)
    normed = group_normalize(hidden_in, totals_attn, count, gain_attn, bias_attn, GROUPS).astype(
        jnp.bfloat16
    )
    query = jnp.dot(normed, w_query, preferred_element_type=jnp.float32).astype(jnp.bfloat16)
    key_fresh = jnp.dot(normed, w_key, preferred_element_type=jnp.float32).astype(jnp.bfloat16)
    value_fresh = jnp.dot(normed, w_value, preferred_element_type=jnp.float32).astype(jnp.bfloat16)
    pieces = []
    for c in range(NCHUNK):
        cols = slice(c * width, (c + 1) * width)
        keys_used = lax.dynamic_update_slice_in_dim(gathered[c][0], key_fresh[:, cols], own_first, 0)
        values_used = lax.dynamic_update_slice_in_dim(
            gathered[c][1], value_fresh[:, cols], own_first, 0
        )
        pieces.append(attention_chunk(query[:, cols], keys_used, values_used, hidden_in, c))
    updated = jnp.concatenate(pieces, axis=1)
    total_conv = lax.psum(own_stale[1], "patch")
    totals_conv = total_conv - own_stale[1] + group_moments(updated, GROUPS)
    normed_conv = group_normalize(updated, totals_conv, count, gain_conv, bias_conv, GROUPS)
    activated = jax.nn.silu(normed_conv).astype(jnp.bfloat16).reshape(tok_rows // W, W, channels)
    padded = padded_2(activated, (("patch", 0),), 1)
    convolved = lax.conv_general_dilated(
        padded[None],
        conv_weight,
        (1, 1),
        ((0, 0), (1, 1)),
        dimension_numbers=("NHWC", "HWIO", "NHWC"),
        preferred_element_type=jnp.float32,
    )[0]
    temb = time_embedding(timestep, w_time)
    conv_out = (convolved + conv_bias + temb).astype(jnp.bfloat16)
    return conv_out.reshape(tok_rows, conv_weight.shape[3])


def solution(mesh):
    return jax.shard_map(
        body,
        mesh=mesh,
        in_specs=(
            P(("batch", "patch"), None),
            P(("batch", "patch"), None),
            P(("batch", "patch"), None),
            P(("batch", "patch"), None, None, None),
            P(),
            P(),
            P(),
            P(),
            P(),
            P(),
            P(),
            P(),
            P(),
            P(),
            P(),
        ),
        out_specs=P(("batch", "patch"), None),
        check_vma=False,
    )
```

```python
import functools
import math

import jax
import jax.numpy as jnp
from jax import lax
from jax.sharding import PartitionSpec as P
from jax.experimental import pallas as pl
from jax.experimental.pallas import tpu as pltpu

HEADS = 20
GROUPS = 32
W = 64
YRING = 4
QBLK = 128


EPS = 1e-05
NEG = -1e30


def padded_2(cells, sides, width):
    for axis, dim in sides:
        count = lax.axis_size(axis)
        ends = count - 1
        head = lax.slice_in_dim(cells, 0, width, axis=dim)
        tail = lax.slice_in_dim(cells, cells.shape[dim] - width, cells.shape[dim], axis=dim)
        cells = jnp.concatenate(
            [
                lax.ppermute(tail, axis, [(i, (i + 1) % count) for i in range(ends)]),
                cells,
                lax.ppermute(head, axis, [((i + 1) % count, i) for i in range(ends)]),
            ],
            axis=dim,
        )
    return cells


def group_moments(rows_in, groups):
    values = rows_in.astype(jnp.float32).reshape(
        rows_in.shape[0], groups, rows_in.shape[1] // groups
    )
    return jnp.stack([jnp.sum(values, axis=(0, 2)), jnp.sum(values * values, axis=(0, 2))])


def group_normalize(rows_in, totals, count, gain, offset, groups):
    average = totals[0] / count
    variance = totals[1] / count - average * average
    inverse = lax.rsqrt(variance + EPS)
    group_width = rows_in.shape[1] // groups
    factors = jnp.repeat(inverse, group_width) * gain
    shifts = offset - jnp.repeat(average * inverse, group_width) * gain
    return rows_in.astype(jnp.float32) * factors + shifts


def time_embedding(timestep, w_time):
    half_dim = w_time.shape[0] // 2
    frequency = jnp.exp(-math.log(10000.0) * jnp.arange(half_dim, dtype=jnp.float32) / half_dim)
    angles = timestep[0].astype(jnp.float32) * frequency
    embedded = jnp.concatenate([jnp.cos(angles), jnp.sin(angles)])
    return jnp.dot(embedded[None, :], w_time.astype(jnp.float32), precision=lax.Precision.HIGHEST)[
        0
    ]


def attn_kernel(*refs, n_pieces):
    q_ref = refs[0]
    piece_refs = refs[1 : 1 + 2 * n_pieces]
    m_ref, l_ref, acc_ref = refs[1 + 2 * n_pieces :]
    head_dim = q_ref.shape[1] // 2
    scale = head_dim ** (-0.5)
    dims = (((1,), (1,)), ((), ()))
    for hh in range(2):
        lanes = slice(hh * head_dim, (hh + 1) * head_dim)
        for qb in range(q_ref.shape[0] // QBLK):
            rows = slice(qb * QBLK, (qb + 1) * QBLK)
            qh = q_ref[rows, lanes]
            m = None
            for i in range(n_pieces):
                s = lax.dot_general(
                    qh, piece_refs[2 * i][:, lanes], dims, preferred_element_type=jnp.float32
                ) * scale
                mi = jnp.max(s, axis=1, keepdims=True)
                m = mi if m is None else jnp.maximum(m, mi)
            total = jnp.zeros_like(m)
            acc = jnp.zeros((QBLK, head_dim), jnp.float32)
            for i in range(n_pieces):
                s = lax.dot_general(
                    qh, piece_refs[2 * i][:, lanes], dims, preferred_element_type=jnp.float32
                ) * scale
                w = jnp.exp(s - m)
                total = total + jnp.sum(w, axis=1, keepdims=True)
                acc = acc + jnp.dot(
                    w.astype(jnp.bfloat16),
                    piece_refs[2 * i + 1][:, lanes],
                    preferred_element_type=jnp.float32,
                )
            m_ref[rows, lanes] = jnp.broadcast_to(m, (QBLK, head_dim))
            l_ref[rows, lanes] = jnp.broadcast_to(total, (QBLK, head_dim))
            acc_ref[rows, lanes] = acc


def attention_partial(query, pieces):
    tok_rows, width = query.shape
    pairs = width // 128
    in_specs = [pl.BlockSpec((tok_rows, 128), lambda h: (0, h))]
    args = [query]
    for keys, kblk, values, vblk in pieces:
        in_specs.append(pl.BlockSpec((keys.shape[0], 128), lambda h, o=kblk: (0, h + o)))
        in_specs.append(pl.BlockSpec((values.shape[0], 128), lambda h, o=vblk: (0, h + o)))
        args += [keys, values]
    out_spec = pl.BlockSpec((tok_rows, 128), lambda h: (0, h))
    out_shape = jax.ShapeDtypeStruct((tok_rows, width), jnp.float32)
    return pl.pallas_call(
        functools.partial(attn_kernel, n_pieces=len(pieces)),
        grid=(pairs,),
        in_specs=in_specs,
        out_specs=[out_spec] * 3,
        out_shape=[out_shape] * 3,
        compiler_params=pltpu.CompilerParams(vmem_limit_bytes=48 * 1024 * 1024),
    )(*args)


def body(
    hidden_in,
    stale_keys,
    stale_values,
    stale_moments,
    gain_attn,
    bias_attn,
    w_query,
    w_key,
    w_value,
    gain_conv,
    bias_conv,
    conv_weight,
    conv_bias,
    w_time,
    timestep,
):
    devices = lax.axis_size("patch")
    tok_rows = hidden_in.shape[0]
    channels = hidden_in.shape[1]
    all_tokens = tok_rows * devices
    count = all_tokens * (channels // GROUPS)
    ring = YRING
    planes = devices // ring
    half = tok_rows // 2
    vblk = channels // 128

    def perm(dy, dz):
        return [
            (z * ring + y, ((z + dz) % planes) * ring + (y + dy) % ring)
            for z in range(planes)
            for y in range(ring)
        ]

    kv = jnp.concatenate([stale_keys, stale_values], axis=1)
    from_left = lax.ppermute(kv, "patch", perm(1, 0))
    from_right = lax.ppermute(kv, "patch", perm(-1, 0))
    partner = lax.ppermute(kv, "patch", perm(0, 1))
    far_a = lax.ppermute(from_left[:half], "patch", perm(1, 0))
    far_b = lax.ppermute(from_right[half:], "patch", perm(-1, 0))
    partner_left = lax.ppermute(partner, "patch", perm(1, 0))
    partner_right = lax.ppermute(partner, "patch", perm(-1, 0))
    partner_far_a = lax.ppermute(partner_left[:half], "patch", perm(1, 0))
    partner_far_b = lax.ppermute(partner_right[half:], "patch", perm(-1, 0))

    own_stale = jnp.sum(stale_moments, axis=0)
    total_attn = lax.psum(own_stale[0], "patch")
    totals_attn = total_attn - own_stale[0] + group_moments(hidden_in, GROUPS)
    normed = group_normalize(hidden_in, totals_attn, count, gain_attn, bias_attn, GROUPS).astype(
        jnp.bfloat16
    )
    query = jnp.dot(normed, w_query, preferred_element_type=jnp.float32).astype(jnp.bfloat16)
    key_fresh = jnp.dot(normed, w_key, preferred_element_type=jnp.float32).astype(jnp.bfloat16)
    value_fresh = jnp.dot(normed, w_value, preferred_element_type=jnp.float32).astype(jnp.bfloat16)

    first = [(key_fresh, 0, value_fresh, 0)] + [
        (a, 0, a, vblk) for a in (from_left, from_right, partner)
    ]
    second = [
        (a, 0, a, vblk)
        for a in (far_a, far_b, partner_left, partner_right, partner_far_a, partner_far_b)
    ]
    m1, l1, acc1 = attention_partial(query, first)
    m2, l2, acc2 = attention_partial(query, second)
    m = jnp.maximum(m1, m2)
    r1 = jnp.exp(m1 - m)
    r2 = jnp.exp(m2 - m)
    attended = (acc1 * r1 + acc2 * r2) / (l1 * r1 + l2 * r2)
    updated = (hidden_in.astype(jnp.float32) + attended).astype(jnp.bfloat16)
    total_conv = lax.psum(own_stale[1], "patch")
    totals_conv = total_conv - own_stale[1] + group_moments(updated, GROUPS)
    normed_conv = group_normalize(updated, totals_conv, count, gain_conv, bias_conv, GROUPS)
    activated = jax.nn.silu(normed_conv).astype(jnp.bfloat16).reshape(tok_rows // W, W, channels)
    padded = padded_2(activated, (("patch", 0),), 1)
    convolved = lax.conv_general_dilated(
        padded[None],
        conv_weight,
        (1, 1),
        ((0, 0), (1, 1)),
        dimension_numbers=("NHWC", "HWIO", "NHWC"),
        preferred_element_type=jnp.float32,
    )[0]
    temb = time_embedding(timestep, w_time)
    conv_out = (convolved + conv_bias + temb).astype(jnp.bfloat16)
    return conv_out.reshape(tok_rows, conv_weight.shape[3])


def solution(mesh):
    return jax.shard_map(
        body,
        mesh=mesh,
        in_specs=(
            P(("batch", "patch"), None),
            P(("batch", "patch"), None),
            P(("batch", "patch"), None),
            P(("batch", "patch"), None, None, None),
            P(),
            P(),
            P(),
            P(),
            P(),
            P(),
            P(),
            P(),
            P(),
            P(),
            P(),
        ),
        out_specs=P(("batch", "patch"), None),
        check_vma=False,
    )
```

```python
import functools
import math

import jax
import jax.numpy as jnp
from jax import lax
from jax.sharding import PartitionSpec as P
from jax.experimental import pallas as pl
from jax.experimental.pallas import tpu as pltpu

HEADS = 20
GROUPS = 32
W = 64
YRING = 4
QBLK = 128


EPS = 1e-05
NEG = -1e30


def padded_2(cells, sides, width):
    for axis, dim in sides:
        count = lax.axis_size(axis)
        ends = count - 1
        head = lax.slice_in_dim(cells, 0, width, axis=dim)
        tail = lax.slice_in_dim(cells, cells.shape[dim] - width, cells.shape[dim], axis=dim)
        cells = jnp.concatenate(
            [
                lax.ppermute(tail, axis, [(i, (i + 1) % count) for i in range(ends)]),
                cells,
                lax.ppermute(head, axis, [((i + 1) % count, i) for i in range(ends)]),
            ],
            axis=dim,
        )
    return cells


def group_moments(rows_in, groups):
    values = rows_in.astype(jnp.float32).reshape(
        rows_in.shape[0], groups, rows_in.shape[1] // groups
    )
    return jnp.stack([jnp.sum(values, axis=(0, 2)), jnp.sum(values * values, axis=(0, 2))])


def group_normalize(rows_in, totals, count, gain, offset, groups):
    average = totals[0] / count
    variance = totals[1] / count - average * average
    inverse = lax.rsqrt(variance + EPS)
    group_width = rows_in.shape[1] // groups
    factors = jnp.repeat(inverse, group_width) * gain
    shifts = offset - jnp.repeat(average * inverse, group_width) * gain
    return rows_in.astype(jnp.float32) * factors + shifts


def time_embedding(timestep, w_time):
    half_dim = w_time.shape[0] // 2
    frequency = jnp.exp(-math.log(10000.0) * jnp.arange(half_dim, dtype=jnp.float32) / half_dim)
    angles = timestep[0].astype(jnp.float32) * frequency
    embedded = jnp.concatenate([jnp.cos(angles), jnp.sin(angles)])
    return jnp.dot(embedded[None, :], w_time.astype(jnp.float32), precision=lax.Precision.HIGHEST)[
        0
    ]


def attn_kernel(*refs, n_pieces):
    q_ref = refs[0]
    piece_refs = refs[1 : 1 + 2 * n_pieces]
    m_ref, l_ref, acc_ref = refs[1 + 2 * n_pieces :]
    head_dim = q_ref.shape[1] // 2
    dims = (((1,), (1,)), ((), ()))
    for hh in range(2):
        lanes = slice(hh * head_dim, (hh + 1) * head_dim)
        qh = q_ref[:, lanes]
        scores = [
            lax.dot_general(
                qh, piece_refs[2 * i][:, lanes], dims, preferred_element_type=jnp.float32
            )
            for i in range(n_pieces)
        ]
        m = functools.reduce(jnp.maximum, [jnp.max(s, axis=1, keepdims=True) for s in scores])
        total = None
        acc = None
        for i in range(n_pieces):
            w = jnp.exp(scores[i] - m)
            part = jnp.sum(w, axis=1, keepdims=True)
            pv = jnp.dot(
                w.astype(jnp.bfloat16),
                piece_refs[2 * i + 1][:, lanes],
                preferred_element_type=jnp.float32,
            )
            total = part if total is None else total + part
            acc = pv if acc is None else acc + pv
        rows = q_ref.shape[0]
        m_ref[:, lanes] = jnp.broadcast_to(m, (rows, head_dim))
        l_ref[:, lanes] = jnp.broadcast_to(total, (rows, head_dim))
        acc_ref[:, lanes] = acc


def attention_partial(query, pieces):
    tok_rows, width = query.shape
    pairs = width // 128
    in_specs = [pl.BlockSpec((tok_rows, 128), lambda h: (0, h))]
    args = [query]
    for keys, kblk, values, vblk in pieces:
        in_specs.append(pl.BlockSpec((keys.shape[0], 128), lambda h, o=kblk: (0, h + o)))
        in_specs.append(pl.BlockSpec((values.shape[0], 128), lambda h, o=vblk: (0, h + o)))
        args += [keys, values]
    out_spec = pl.BlockSpec((tok_rows, 128), lambda h: (0, h))
    out_shape = jax.ShapeDtypeStruct((tok_rows, width), jnp.float32)
    return pl.pallas_call(
        functools.partial(attn_kernel, n_pieces=len(pieces)),
        grid=(pairs,),
        in_specs=in_specs,
        out_specs=[out_spec] * 3,
        out_shape=[out_shape] * 3,
        compiler_params=pltpu.CompilerParams(vmem_limit_bytes=48 * 1024 * 1024),
    )(*args)


def body(
    hidden_in,
    stale_keys,
    stale_values,
    stale_moments,
    gain_attn,
    bias_attn,
    w_query,
    w_key,
    w_value,
    gain_conv,
    bias_conv,
    conv_weight,
    conv_bias,
    w_time,
    timestep,
):
    devices = lax.axis_size("patch")
    tok_rows = hidden_in.shape[0]
    channels = hidden_in.shape[1]
    all_tokens = tok_rows * devices
    count = all_tokens * (channels // GROUPS)
    ring = YRING
    planes = devices // ring
    half = tok_rows // 2
    vblk = channels // 128

    def perm(dy, dz):
        return [
            (z * ring + y, ((z + dz) % planes) * ring + (y + dy) % ring)
            for z in range(planes)
            for y in range(ring)
        ]

    own_stale = jnp.sum(stale_moments, axis=0)
    stale_all = lax.psum(own_stale, "patch")
    kv = jnp.concatenate([stale_keys, stale_values], axis=1)
    kv, stale_all = lax.optimization_barrier((kv, stale_all))
    from_left = lax.ppermute(kv, "patch", perm(1, 0))
    from_right = lax.ppermute(kv, "patch", perm(-1, 0))
    partner = lax.ppermute(kv, "patch", perm(0, 1))
    far_a = lax.ppermute(from_left[:half], "patch", perm(1, 0))
    far_b = lax.ppermute(from_right[half:], "patch", perm(-1, 0))
    partner_left = lax.ppermute(partner, "patch", perm(1, 0))
    partner_right = lax.ppermute(partner, "patch", perm(-1, 0))
    partner_far_a = lax.ppermute(partner_left[:half], "patch", perm(1, 0))
    partner_far_b = lax.ppermute(partner_right[half:], "patch", perm(-1, 0))

    total_attn = stale_all[0]
    totals_attn = total_attn - own_stale[0] + group_moments(hidden_in, GROUPS)
    normed = group_normalize(hidden_in, totals_attn, count, gain_attn, bias_attn, GROUPS).astype(
        jnp.bfloat16
    )
    query = jnp.dot(normed, w_query, preferred_element_type=jnp.float32).astype(jnp.bfloat16)
    key_fresh = jnp.dot(normed, w_key, preferred_element_type=jnp.float32).astype(jnp.bfloat16)
    value_fresh = jnp.dot(normed, w_value, preferred_element_type=jnp.float32).astype(jnp.bfloat16)

    first = [(key_fresh, 0, value_fresh, 0)] + [
        (a, 0, a, vblk) for a in (from_left, from_right, partner)
    ]
    second = [
        (a, 0, a, vblk)
        for a in (far_a, far_b, partner_left, partner_right, partner_far_a, partner_far_b)
    ]
    query = query * jnp.asarray((channels // HEADS) ** -0.5, jnp.bfloat16)
    m1, l1, acc1 = attention_partial(query, first)
    m2, l2, acc2 = attention_partial(query, second)
    m = jnp.maximum(m1, m2)
    r1 = jnp.exp(m1 - m)
    r2 = jnp.exp(m2 - m)
    attended = (acc1 * r1 + acc2 * r2) / (l1 * r1 + l2 * r2)
    updated = (hidden_in.astype(jnp.float32) + attended).astype(jnp.bfloat16)
    total_conv = stale_all[1]
    totals_conv = total_conv - own_stale[1] + group_moments(updated, GROUPS)
    normed_conv = group_normalize(updated, totals_conv, count, gain_conv, bias_conv, GROUPS)
    activated = jax.nn.silu(normed_conv).astype(jnp.bfloat16).reshape(tok_rows // W, W, channels)
    padded = padded_2(activated, (("patch", 0),), 1)
    convolved = lax.conv_general_dilated(
        padded[None],
        conv_weight,
        (1, 1),
        ((0, 0), (1, 1)),
        dimension_numbers=("NHWC", "HWIO", "NHWC"),
        preferred_element_type=jnp.float32,
    )[0]
    temb = time_embedding(timestep, w_time)
    conv_out = (convolved + conv_bias + temb).astype(jnp.bfloat16)
    return conv_out.reshape(tok_rows, conv_weight.shape[3])


def solution(mesh):
    return jax.shard_map(
        body,
        mesh=mesh,
        in_specs=(
            P(("batch", "patch"), None),
            P(("batch", "patch"), None),
            P(("batch", "patch"), None),
            P(("batch", "patch"), None, None, None),
            P(),
            P(),
            P(),
            P(),
            P(),
            P(),
            P(),
            P(),
            P(),
            P(),
            P(),
        ),
        out_specs=P(("batch", "patch"), None),
        check_vma=False,
    )
```

```python
import functools
import math

import jax
import jax.numpy as jnp
from jax import lax
from jax.sharding import PartitionSpec as P
from jax.experimental import pallas as pl
from jax.experimental.pallas import tpu as pltpu

HEADS = 20
GROUPS = 32
W = 64
YRING = 4


EPS = 1e-05


def padded_2(cells, sides, width):
    for axis, dim in sides:
        count = lax.axis_size(axis)
        ends = count - 1
        head = lax.slice_in_dim(cells, 0, width, axis=dim)
        tail = lax.slice_in_dim(cells, cells.shape[dim] - width, cells.shape[dim], axis=dim)
        cells = jnp.concatenate(
            [
                lax.ppermute(tail, axis, [(i, (i + 1) % count) for i in range(ends)]),
                cells,
                lax.ppermute(head, axis, [((i + 1) % count, i) for i in range(ends)]),
            ],
            axis=dim,
        )
    return cells


def group_moments(rows_in, groups):
    values = rows_in.astype(jnp.float32).reshape(
        rows_in.shape[0], groups, rows_in.shape[1] // groups
    )
    return jnp.stack([jnp.sum(values, axis=(0, 2)), jnp.sum(values * values, axis=(0, 2))])


def group_normalize(rows_in, totals, count, gain, offset, groups):
    average = totals[0] / count
    variance = totals[1] / count - average * average
    inverse = lax.rsqrt(variance + EPS)
    group_width = rows_in.shape[1] // groups
    factors = jnp.repeat(inverse, group_width) * gain
    shifts = offset - jnp.repeat(average * inverse, group_width) * gain
    return rows_in.astype(jnp.float32) * factors + shifts


def time_embedding(timestep, w_time):
    half_dim = w_time.shape[0] // 2
    frequency = jnp.exp(-math.log(10000.0) * jnp.arange(half_dim, dtype=jnp.float32) / half_dim)
    angles = timestep[0].astype(jnp.float32) * frequency
    embedded = jnp.concatenate([jnp.cos(angles), jnp.sin(angles)])
    return jnp.dot(embedded[None, :], w_time.astype(jnp.float32), precision=lax.Precision.HIGHEST)[
        0
    ]


def attn_kernel(*refs, n_pieces):
    q_ref = refs[0]
    piece_refs = refs[1 : 1 + 2 * n_pieces]
    m_ref, l_ref, acc_ref = refs[1 + 2 * n_pieces :]
    head_dim = q_ref.shape[1] // 2
    dims = (((1,), (1,)), ((), ()))
    for hh in range(2):
        lanes = slice(hh * head_dim, (hh + 1) * head_dim)
        qh = q_ref[:, lanes]
        scores = [
            lax.dot_general(
                qh, piece_refs[2 * i][:, lanes], dims, preferred_element_type=jnp.float32
            )
            for i in range(n_pieces)
        ]
        m = functools.reduce(jnp.maximum, [jnp.max(s, axis=1, keepdims=True) for s in scores])
        total = None
        acc = None
        for i in range(n_pieces):
            w = jnp.exp(scores[i] - m)
            part = jnp.sum(w, axis=1, keepdims=True)
            pv = jnp.dot(
                w.astype(jnp.bfloat16),
                piece_refs[2 * i + 1][:, lanes],
                preferred_element_type=jnp.float32,
            )
            total = part if total is None else total + part
            acc = pv if acc is None else acc + pv
        rows = q_ref.shape[0]
        m_ref[:, lanes] = jnp.broadcast_to(m, (rows, head_dim))
        l_ref[:, lanes] = jnp.broadcast_to(total, (rows, head_dim))
        acc_ref[:, lanes] = acc


def attention_partial(query, pieces):
    tok_rows, width = query.shape
    pairs = width // 128
    in_specs = [pl.BlockSpec((tok_rows, 128), lambda h: (0, h))]
    args = [query]
    for keys, kblk, values, vblk in pieces:
        in_specs.append(pl.BlockSpec((keys.shape[0], 128), lambda h, o=kblk: (0, h + o)))
        in_specs.append(pl.BlockSpec((values.shape[0], 128), lambda h, o=vblk: (0, h + o)))
        args += [keys, values]
    out_spec = pl.BlockSpec((tok_rows, 128), lambda h: (0, h))
    out_shape = jax.ShapeDtypeStruct((tok_rows, width), jnp.float32)
    return pl.pallas_call(
        functools.partial(attn_kernel, n_pieces=len(pieces)),
        grid=(pairs,),
        in_specs=in_specs,
        out_specs=[out_spec] * 3,
        out_shape=[out_shape] * 3,
        compiler_params=pltpu.CompilerParams(vmem_limit_bytes=48 * 1024 * 1024),
    )(*args)


def body(
    hidden_in,
    stale_keys,
    stale_values,
    stale_moments,
    gain_attn,
    bias_attn,
    w_query,
    w_key,
    w_value,
    gain_conv,
    bias_conv,
    conv_weight,
    conv_bias,
    w_time,
    timestep,
):
    devices = lax.axis_size("patch")
    tok_rows = hidden_in.shape[0]
    channels = hidden_in.shape[1]
    all_tokens = tok_rows * devices
    count = all_tokens * (channels // GROUPS)
    ring = YRING
    planes = devices // ring
    half = tok_rows // 2
    vblk = channels // 128

    def perm(dy, dz):
        return [
            (z * ring + y, ((z + dz) % planes) * ring + (y + dy) % ring)
            for z in range(planes)
            for y in range(ring)
        ]

    own_stale = jnp.sum(stale_moments, axis=0)
    stale_all = own_stale
    for flip in range(1, ring):
        if flip & (flip - 1) == 0:
            pairs = [
                (z * ring + y, z * ring + (y ^ flip)) for z in range(planes) for y in range(ring)
            ]
            stale_all = stale_all + lax.ppermute(stale_all, "patch", pairs)
    stale_all = stale_all + lax.ppermute(stale_all, "patch", perm(0, 1))
    kv = jnp.concatenate([stale_keys, stale_values], axis=1)
    kv, stale_all = lax.optimization_barrier((kv, stale_all))
    from_left = lax.ppermute(kv, "patch", perm(1, 0))
    from_right = lax.ppermute(kv, "patch", perm(-1, 0))
    partner = lax.ppermute(kv, "patch", perm(0, 1))
    far_a = lax.ppermute(from_left[:half], "patch", perm(1, 0))
    far_b = lax.ppermute(from_right[half:], "patch", perm(-1, 0))
    partner_left = lax.ppermute(partner, "patch", perm(1, 0))
    partner_right = lax.ppermute(partner, "patch", perm(-1, 0))
    partner_far_a = lax.ppermute(partner_left[:half], "patch", perm(1, 0))
    partner_far_b = lax.ppermute(partner_right[half:], "patch", perm(-1, 0))

    total_attn = stale_all[0]
    totals_attn = total_attn - own_stale[0] + group_moments(hidden_in, GROUPS)
    normed = group_normalize(hidden_in, totals_attn, count, gain_attn, bias_attn, GROUPS).astype(
        jnp.bfloat16
    )
    query = jnp.dot(normed, w_query, preferred_element_type=jnp.float32).astype(jnp.bfloat16)
    key_fresh = jnp.dot(normed, w_key, preferred_element_type=jnp.float32).astype(jnp.bfloat16)
    value_fresh = jnp.dot(normed, w_value, preferred_element_type=jnp.float32).astype(jnp.bfloat16)
    query = query * jnp.asarray((channels // HEADS) ** -0.5, jnp.bfloat16)

    sets = [
        [(key_fresh, 0, value_fresh, 0)]
        + [(a, 0, a, vblk) for a in (from_left, from_right, partner)],
        [(a, 0, a, vblk) for a in (far_a, far_b, partner_left, partner_right)],
        [(a, 0, a, vblk) for a in (partner_far_a, partner_far_b)],
    ]
    partials = []
    for pieces in sets:
        partials.append(attention_partial(query, pieces))
    m = functools.reduce(jnp.maximum, [p[0] for p in partials])
    scales = [jnp.exp(p[0] - m) for p in partials]
    acc = sum(p[2] * r for p, r in zip(partials, scales))
    total = sum(p[1] * r for p, r in zip(partials, scales))
    attended = acc / total
    updated = (hidden_in.astype(jnp.float32) + attended).astype(jnp.bfloat16)
    total_conv = stale_all[1]
    totals_conv = total_conv - own_stale[1] + group_moments(updated, GROUPS)
    normed_conv = group_normalize(updated, totals_conv, count, gain_conv, bias_conv, GROUPS)
    activated = jax.nn.silu(normed_conv).astype(jnp.bfloat16).reshape(tok_rows // W, W, channels)
    padded = padded_2(activated, (("patch", 0),), 1)
    convolved = lax.conv_general_dilated(
        padded[None],
        conv_weight,
        (1, 1),
        ((0, 0), (1, 1)),
        dimension_numbers=("NHWC", "HWIO", "NHWC"),
        preferred_element_type=jnp.float32,
    )[0]
    temb = time_embedding(timestep, w_time)
    conv_out = (convolved + conv_bias + temb).astype(jnp.bfloat16)
    return conv_out.reshape(tok_rows, conv_weight.shape[3])


def solution(mesh):
    return jax.shard_map(
        body,
        mesh=mesh,
        in_specs=(
            P(("batch", "patch"), None),
            P(("batch", "patch"), None),
            P(("batch", "patch"), None),
            P(("batch", "patch"), None, None, None),
            P(),
            P(),
            P(),
            P(),
            P(),
            P(),
            P(),
            P(),
            P(),
            P(),
            P(),
        ),
        out_specs=P(("batch", "patch"), None),
        check_vma=False,
    )
```

```python
import functools
import math

import jax
import jax.numpy as jnp
from jax import lax
from jax.sharding import PartitionSpec as P
from jax.experimental import pallas as pl
from jax.experimental.pallas import tpu as pltpu

HEADS = 20
GROUPS = 32
W = 64
YRING = 4


EPS = 1e-05


def padded_2(cells, sides, width):
    for axis, dim in sides:
        count = lax.axis_size(axis)
        ends = count - 1
        head = lax.slice_in_dim(cells, 0, width, axis=dim)
        tail = lax.slice_in_dim(cells, cells.shape[dim] - width, cells.shape[dim], axis=dim)
        cells = jnp.concatenate(
            [
                lax.ppermute(tail, axis, [(i, (i + 1) % count) for i in range(ends)]),
                cells,
                lax.ppermute(head, axis, [((i + 1) % count, i) for i in range(ends)]),
            ],
            axis=dim,
        )
    return cells


def group_moments(rows_in, groups):
    values = rows_in.astype(jnp.float32).reshape(
        rows_in.shape[0], groups, rows_in.shape[1] // groups
    )
    return jnp.stack([jnp.sum(values, axis=(0, 2)), jnp.sum(values * values, axis=(0, 2))])


def group_normalize(rows_in, totals, count, gain, offset, groups):
    average = totals[0] / count
    variance = totals[1] / count - average * average
    inverse = lax.rsqrt(variance + EPS)
    group_width = rows_in.shape[1] // groups
    factors = jnp.repeat(inverse, group_width) * gain
    shifts = offset - jnp.repeat(average * inverse, group_width) * gain
    return rows_in.astype(jnp.float32) * factors + shifts


def time_embedding(timestep, w_time):
    half_dim = w_time.shape[0] // 2
    frequency = jnp.exp(-math.log(10000.0) * jnp.arange(half_dim, dtype=jnp.float32) / half_dim)
    angles = timestep[0].astype(jnp.float32) * frequency
    embedded = jnp.concatenate([jnp.cos(angles), jnp.sin(angles)])
    return jnp.dot(embedded[None, :], w_time.astype(jnp.float32), precision=lax.Precision.HIGHEST)[
        0
    ]


def attn_kernel(*refs, n_pieces):
    q_ref = refs[0]
    piece_refs = refs[1 : 1 + 2 * n_pieces]
    m_ref, l_ref, acc_ref = refs[1 + 2 * n_pieces :]
    head_dim = q_ref.shape[1] // 2
    dims = (((1,), (1,)), ((), ()))
    for hh in range(2):
        lanes = slice(hh * head_dim, (hh + 1) * head_dim)
        qh = q_ref[:, lanes]
        scores = [
            lax.dot_general(
                qh, piece_refs[2 * i][:, lanes], dims, preferred_element_type=jnp.float32
            )
            for i in range(n_pieces)
        ]
        m = functools.reduce(jnp.maximum, [jnp.max(s, axis=1, keepdims=True) for s in scores])
        total = None
        acc = None
        for i in range(n_pieces):
            w = jnp.exp(scores[i] - m)
            part = jnp.sum(w, axis=1, keepdims=True)
            pv = jnp.dot(
                w.astype(jnp.bfloat16),
                piece_refs[2 * i + 1][:, lanes],
                preferred_element_type=jnp.float32,
            )
            total = part if total is None else total + part
            acc = pv if acc is None else acc + pv
        rows = q_ref.shape[0]
        m_ref[:, lanes] = jnp.broadcast_to(m, (rows, head_dim))
        l_ref[:, lanes] = jnp.broadcast_to(total, (rows, head_dim))
        acc_ref[:, lanes] = acc


def attention_partial(query, pieces):
    tok_rows, width = query.shape
    pairs = width // 128
    in_specs = [pl.BlockSpec((tok_rows, 128), lambda h: (0, h))]
    args = [query]
    for keys, kblk, values, vblk in pieces:
        in_specs.append(pl.BlockSpec((keys.shape[0], 128), lambda h, o=kblk: (0, h + o)))
        in_specs.append(pl.BlockSpec((values.shape[0], 128), lambda h, o=vblk: (0, h + o)))
        args += [keys, values]
    out_spec = pl.BlockSpec((tok_rows, 128), lambda h: (0, h))
    out_shape = jax.ShapeDtypeStruct((tok_rows, width), jnp.float32)
    return pl.pallas_call(
        functools.partial(attn_kernel, n_pieces=len(pieces)),
        grid=(pairs,),
        in_specs=in_specs,
        out_specs=[out_spec] * 3,
        out_shape=[out_shape] * 3,
        compiler_params=pltpu.CompilerParams(vmem_limit_bytes=48 * 1024 * 1024),
    )(*args)


def body(
    hidden_in,
    stale_keys,
    stale_values,
    stale_moments,
    gain_attn,
    bias_attn,
    w_query,
    w_key,
    w_value,
    gain_conv,
    bias_conv,
    conv_weight,
    conv_bias,
    w_time,
    timestep,
):
    devices = lax.axis_size("patch")
    tok_rows = hidden_in.shape[0]
    channels = hidden_in.shape[1]
    all_tokens = tok_rows * devices
    count = all_tokens * (channels // GROUPS)
    ring = YRING
    planes = devices // ring
    half = tok_rows // 2
    vblk = channels // 128

    def perm(dy, dz):
        return [
            (z * ring + y, ((z + dz) % planes) * ring + (y + dy) % ring)
            for z in range(planes)
            for y in range(ring)
        ]

    own_stale = jnp.sum(stale_moments, axis=0)
    stale_all = own_stale
    for flip in range(1, ring):
        if flip & (flip - 1) == 0:
            pairs = [
                (z * ring + y, z * ring + (y ^ flip)) for z in range(planes) for y in range(ring)
            ]
            stale_all = stale_all + lax.ppermute(stale_all, "patch", pairs)
    stale_all = stale_all + lax.ppermute(stale_all, "patch", perm(0, 1))
    kv = jnp.concatenate([stale_keys, stale_values], axis=1)
    from_left = lax.ppermute(kv, "patch", perm(1, 0))
    from_right = lax.ppermute(kv, "patch", perm(-1, 0))
    partner = lax.ppermute(kv, "patch", perm(0, 1))
    far_a = lax.ppermute(from_left[:half], "patch", perm(1, 0))
    far_b = lax.ppermute(from_right[half:], "patch", perm(-1, 0))
    partner_left = lax.ppermute(from_left, "patch", perm(0, 1))
    partner_right = lax.ppermute(partner, "patch", perm(-1, 0))
    partner_far_a = lax.ppermute(partner_left[:half], "patch", perm(1, 0))
    partner_far_b = lax.ppermute(partner_right[half:], "patch", perm(-1, 0))

    total_attn = stale_all[0]
    totals_attn = total_attn - own_stale[0] + group_moments(hidden_in, GROUPS)
    normed = group_normalize(hidden_in, totals_attn, count, gain_attn, bias_attn, GROUPS).astype(
        jnp.bfloat16
    )
    query = jnp.dot(normed, w_query, preferred_element_type=jnp.float32).astype(jnp.bfloat16)
    key_fresh = jnp.dot(normed, w_key, preferred_element_type=jnp.float32).astype(jnp.bfloat16)
    value_fresh = jnp.dot(normed, w_value, preferred_element_type=jnp.float32).astype(jnp.bfloat16)
    query = query * jnp.asarray((channels // HEADS) ** -0.5, jnp.bfloat16)

    far = jnp.concatenate([far_a, far_b], axis=0)
    partner_far = jnp.concatenate([partner_far_a, partner_far_b], axis=0)
    sets = [
        [(key_fresh, 0, value_fresh, 0)]
        + [(a, 0, a, vblk) for a in (from_left, from_right, partner)],
        [(a, 0, a, vblk) for a in (far, partner_left, partner_right)],
        [(partner_far, 0, partner_far, vblk)],
    ]
    partials = []
    for pieces in sets:
        partials.append(attention_partial(query, pieces))
    m = functools.reduce(jnp.maximum, [p[0] for p in partials])
    scales = [jnp.exp(p[0] - m) for p in partials]
    acc = sum(p[2] * r for p, r in zip(partials, scales))
    total = sum(p[1] * r for p, r in zip(partials, scales))
    attended = acc / total
    updated = (hidden_in.astype(jnp.float32) + attended).astype(jnp.bfloat16)
    total_conv = stale_all[1]
    totals_conv = total_conv - own_stale[1] + group_moments(updated, GROUPS)
    normed_conv = group_normalize(updated, totals_conv, count, gain_conv, bias_conv, GROUPS)
    activated = jax.nn.silu(normed_conv).astype(jnp.bfloat16).reshape(tok_rows // W, W, channels)
    padded = padded_2(activated, (("patch", 0),), 1)
    convolved = lax.conv_general_dilated(
        padded[None],
        conv_weight,
        (1, 1),
        ((0, 0), (1, 1)),
        dimension_numbers=("NHWC", "HWIO", "NHWC"),
        preferred_element_type=jnp.float32,
    )[0]
    temb = time_embedding(timestep, w_time)
    conv_out = (convolved + conv_bias + temb).astype(jnp.bfloat16)
    return conv_out.reshape(tok_rows, conv_weight.shape[3])


def solution(mesh):
    return jax.shard_map(
        body,
        mesh=mesh,
        in_specs=(
            P(("batch", "patch"), None),
            P(("batch", "patch"), None),
            P(("batch", "patch"), None),
            P(("batch", "patch"), None, None, None),
            P(),
            P(),
            P(),
            P(),
            P(),
            P(),
            P(),
            P(),
            P(),
            P(),
            P(),
        ),
        out_specs=P(("batch", "patch"), None),
        check_vma=False,
    )
```

```python
import functools
import math

import jax
import jax.numpy as jnp
from jax import lax
from jax.sharding import PartitionSpec as P
from jax.experimental import pallas as pl
from jax.experimental.pallas import tpu as pltpu

HEADS = 20
GROUPS = 32
W = 64
YRING = 4
SC_PAIRS = 4


EPS = 1e-05


def padded_2(cells, sides, width):
    for axis, dim in sides:
        count = lax.axis_size(axis)
        ends = count - 1
        head = lax.slice_in_dim(cells, 0, width, axis=dim)
        tail = lax.slice_in_dim(cells, cells.shape[dim] - width, cells.shape[dim], axis=dim)
        cells = jnp.concatenate(
            [
                lax.ppermute(tail, axis, [(i, (i + 1) % count) for i in range(ends)]),
                cells,
                lax.ppermute(head, axis, [((i + 1) % count, i) for i in range(ends)]),
            ],
            axis=dim,
        )
    return cells


def group_moments(rows_in, groups):
    values = rows_in.astype(jnp.float32).reshape(
        rows_in.shape[0], groups, rows_in.shape[1] // groups
    )
    return jnp.stack([jnp.sum(values, axis=(0, 2)), jnp.sum(values * values, axis=(0, 2))])


def group_normalize(rows_in, totals, count, gain, offset, groups):
    average = totals[0] / count
    variance = totals[1] / count - average * average
    inverse = lax.rsqrt(variance + EPS)
    group_width = rows_in.shape[1] // groups
    factors = jnp.repeat(inverse, group_width) * gain
    shifts = offset - jnp.repeat(average * inverse, group_width) * gain
    return rows_in.astype(jnp.float32) * factors + shifts


def time_embedding(timestep, w_time):
    half_dim = w_time.shape[0] // 2
    frequency = jnp.exp(-math.log(10000.0) * jnp.arange(half_dim, dtype=jnp.float32) / half_dim)
    angles = timestep[0].astype(jnp.float32) * frequency
    embedded = jnp.concatenate([jnp.cos(angles), jnp.sin(angles)])
    return jnp.dot(embedded[None, :], w_time.astype(jnp.float32), precision=lax.Precision.HIGHEST)[
        0
    ]


def attn_kernel(*refs, n_pieces):
    q_ref = refs[0]
    piece_refs = refs[1 : 1 + 2 * n_pieces]
    m_ref, l_ref, acc_ref = refs[1 + 2 * n_pieces :]
    head_dim = q_ref.shape[1] // 2
    dims = (((1,), (1,)), ((), ()))
    for hh in range(2):
        lanes = slice(hh * head_dim, (hh + 1) * head_dim)
        qh = q_ref[:, lanes]
        scores = [
            lax.dot_general(
                qh, piece_refs[2 * i][:, lanes], dims, preferred_element_type=jnp.float32
            )
            for i in range(n_pieces)
        ]
        m = functools.reduce(jnp.maximum, [jnp.max(s, axis=1, keepdims=True) for s in scores])
        total = None
        acc = None
        for i in range(n_pieces):
            w = jnp.exp(scores[i] - m)
            part = jnp.sum(w, axis=1, keepdims=True)
            pv = jnp.dot(
                w.astype(jnp.bfloat16),
                piece_refs[2 * i + 1][:, lanes],
                preferred_element_type=jnp.float32,
            )
            total = part if total is None else total + part
            acc = pv if acc is None else acc + pv
        rows = q_ref.shape[0]
        m_ref[:, lanes] = jnp.broadcast_to(m, (rows, head_dim))
        l_ref[:, lanes] = jnp.broadcast_to(total, (rows, head_dim))
        acc_ref[:, lanes] = acc


def attention_partial(query, pieces):
    tok_rows, width = query.shape
    pairs = width // 128
    in_specs = [pl.BlockSpec((tok_rows, 128), lambda h: (0, h))]
    args = [query]
    for keys, kblk, values, vblk in pieces:
        in_specs.append(pl.BlockSpec((keys.shape[0], 128), lambda h, o=kblk: (0, h + o)))
        in_specs.append(pl.BlockSpec((values.shape[0], 128), lambda h, o=vblk: (0, h + o)))
        args += [keys, values]
    out_spec = pl.BlockSpec((tok_rows, 128), lambda h: (0, h))
    out_shape = jax.ShapeDtypeStruct((tok_rows, width), jnp.float32)
    return pl.pallas_call(
        functools.partial(attn_kernel, n_pieces=len(pieces)),
        grid=(pairs,),
        in_specs=in_specs,
        out_specs=[out_spec] * 3,
        out_shape=[out_shape] * 3,
        compiler_params=pltpu.CompilerParams(vmem_limit_bytes=48 * 1024 * 1024),
    )(*args)


def body(
    hidden_in,
    stale_keys,
    stale_values,
    stale_moments,
    gain_attn,
    bias_attn,
    w_query,
    w_key,
    w_value,
    gain_conv,
    bias_conv,
    conv_weight,
    conv_bias,
    w_time,
    timestep,
):
    devices = lax.axis_size("patch")
    tok_rows = hidden_in.shape[0]
    channels = hidden_in.shape[1]
    all_tokens = tok_rows * devices
    count = all_tokens * (channels // GROUPS)
    ring = YRING
    planes = devices // ring
    half = tok_rows // 2
    vblk = channels // 128 - SC_PAIRS

    def perm(dy, dz):
        return [
            (z * ring + y, ((z + dz) % planes) * ring + (y + dy) % ring)
            for z in range(planes)
            for y in range(ring)
        ]

    own_stale = jnp.sum(stale_moments, axis=0)
    stale_all = own_stale
    for flip in range(1, ring):
        if flip & (flip - 1) == 0:
            pairs = [
                (z * ring + y, z * ring + (y ^ flip)) for z in range(planes) for y in range(ring)
            ]
            stale_all = stale_all + lax.ppermute(stale_all, "patch", pairs)
    stale_all = stale_all + lax.ppermute(stale_all, "patch", perm(0, 1))
    split = SC_PAIRS * 128
    kv_sc = jnp.concatenate([stale_keys[:, :split], stale_values[:, :split]], axis=1)
    gathered = lax.all_gather(kv_sc, "patch", axis=0, tiled=True)
    kv = jnp.concatenate([stale_keys[:, split:], stale_values[:, split:]], axis=1)
    from_left = lax.ppermute(kv, "patch", perm(1, 0))
    from_right = lax.ppermute(kv, "patch", perm(-1, 0))
    partner = lax.ppermute(kv, "patch", perm(0, 1))
    far_a = lax.ppermute(from_left[:half], "patch", perm(1, 0))
    far_b = lax.ppermute(from_right[half:], "patch", perm(-1, 0))
    partner_left = lax.ppermute(from_left, "patch", perm(0, 1))
    partner_right = lax.ppermute(partner, "patch", perm(-1, 0))
    partner_far_a = lax.ppermute(partner_left[:half], "patch", perm(1, 0))
    partner_far_b = lax.ppermute(partner_right[half:], "patch", perm(-1, 0))

    total_attn = stale_all[0]
    totals_attn = total_attn - own_stale[0] + group_moments(hidden_in, GROUPS)
    normed = group_normalize(hidden_in, totals_attn, count, gain_attn, bias_attn, GROUPS).astype(
        jnp.bfloat16
    )
    query = jnp.dot(normed, w_query, preferred_element_type=jnp.float32).astype(jnp.bfloat16)
    key_fresh = jnp.dot(normed, w_key, preferred_element_type=jnp.float32).astype(jnp.bfloat16)
    value_fresh = jnp.dot(normed, w_value, preferred_element_type=jnp.float32).astype(jnp.bfloat16)
    query = query * jnp.asarray((channels // HEADS) ** -0.5, jnp.bfloat16)

    far = jnp.concatenate([far_a, far_b], axis=0)
    partner_far = jnp.concatenate([partner_far_a, partner_far_b], axis=0)
    query_tc = query[:, split:]
    sets = [
        [(key_fresh[:, split:], 0, value_fresh[:, split:], 0)]
        + [(a, 0, a, vblk) for a in (from_left, from_right, partner)],
        [(a, 0, a, vblk) for a in (far, partner_left, partner_right)],
        [(partner_far, 0, partner_far, vblk)],
    ]
    partials = []
    for pieces in sets:
        partials.append(attention_partial(query_tc, pieces))
    m = functools.reduce(jnp.maximum, [p[0] for p in partials])
    scales = [jnp.exp(p[0] - m) for p in partials]
    acc = sum(p[2] * r for p, r in zip(partials, scales))
    total = sum(p[1] * r for p, r in zip(partials, scales))
    own_first = lax.axis_index("patch") * tok_rows
    fresh_sc = jnp.concatenate([key_fresh[:, :split], value_fresh[:, :split]], axis=1)
    keys_sc = lax.dynamic_update_slice_in_dim(gathered, fresh_sc, own_first, 0)
    _, l_sc, acc_sc = attention_partial(query[:, :split], [(keys_sc, 0, keys_sc, SC_PAIRS)])
    attended = jnp.concatenate([acc_sc / l_sc, acc / total], axis=1)
    updated = (hidden_in.astype(jnp.float32) + attended).astype(jnp.bfloat16)
    total_conv = stale_all[1]
    totals_conv = total_conv - own_stale[1] + group_moments(updated, GROUPS)
    normed_conv = group_normalize(updated, totals_conv, count, gain_conv, bias_conv, GROUPS)
    activated = jax.nn.silu(normed_conv).astype(jnp.bfloat16).reshape(tok_rows // W, W, channels)
    padded = padded_2(activated, (("patch", 0),), 1)
    convolved = lax.conv_general_dilated(
        padded[None],
        conv_weight,
        (1, 1),
        ((0, 0), (1, 1)),
        dimension_numbers=("NHWC", "HWIO", "NHWC"),
        preferred_element_type=jnp.float32,
    )[0]
    temb = time_embedding(timestep, w_time)
    conv_out = (convolved + conv_bias + temb).astype(jnp.bfloat16)
    return conv_out.reshape(tok_rows, conv_weight.shape[3])


def solution(mesh):
    return jax.shard_map(
        body,
        mesh=mesh,
        in_specs=(
            P(("batch", "patch"), None),
            P(("batch", "patch"), None),
            P(("batch", "patch"), None),
            P(("batch", "patch"), None, None, None),
            P(),
            P(),
            P(),
            P(),
            P(),
            P(),
            P(),
            P(),
            P(),
            P(),
            P(),
        ),
        out_specs=P(("batch", "patch"), None),
        check_vma=False,
    )
```

```python
import functools
import math

import jax
import jax.numpy as jnp
from jax import lax
from jax.sharding import PartitionSpec as P
from jax.experimental import pallas as pl
from jax.experimental.pallas import tpu as pltpu

HEADS = 20
GROUPS = 32
W = 64
YRING = 4


EPS = 1e-05


def group_moments(rows_in, groups):
    values = rows_in.astype(jnp.float32).reshape(
        rows_in.shape[0], groups, rows_in.shape[1] // groups
    )
    return jnp.stack([jnp.sum(values, axis=(0, 2)), jnp.sum(values * values, axis=(0, 2))])


def group_normalize(rows_in, totals, count, gain, offset, groups):
    average = totals[0] / count
    variance = totals[1] / count - average * average
    inverse = lax.rsqrt(variance + EPS)
    group_width = rows_in.shape[1] // groups
    factors = jnp.repeat(inverse, group_width) * gain
    shifts = offset - jnp.repeat(average * inverse, group_width) * gain
    return rows_in.astype(jnp.float32) * factors + shifts


def time_embedding(timestep, w_time):
    half_dim = w_time.shape[0] // 2
    frequency = jnp.exp(-math.log(10000.0) * jnp.arange(half_dim, dtype=jnp.float32) / half_dim)
    angles = timestep[0].astype(jnp.float32) * frequency
    embedded = jnp.concatenate([jnp.cos(angles), jnp.sin(angles)])
    return jnp.dot(embedded[None, :], w_time.astype(jnp.float32), precision=lax.Precision.HIGHEST)[
        0
    ]


def attn_kernel(*refs, n_pieces):
    q_ref = refs[0]
    piece_refs = refs[1 : 1 + 2 * n_pieces]
    m_ref, l_ref, acc_ref = refs[1 + 2 * n_pieces :]
    head_dim = q_ref.shape[1] // 2
    dims = (((1,), (1,)), ((), ()))
    for hh in range(2):
        lanes = slice(hh * head_dim, (hh + 1) * head_dim)
        qh = q_ref[:, lanes]
        scores = [
            lax.dot_general(
                qh, piece_refs[2 * i][:, lanes], dims, preferred_element_type=jnp.float32
            )
            for i in range(n_pieces)
        ]
        m = functools.reduce(jnp.maximum, [jnp.max(s, axis=1, keepdims=True) for s in scores])
        total = None
        acc = None
        for i in range(n_pieces):
            w = jnp.exp(scores[i] - m)
            part = jnp.sum(w, axis=1, keepdims=True)
            pv = jnp.dot(
                w.astype(jnp.bfloat16),
                piece_refs[2 * i + 1][:, lanes],
                preferred_element_type=jnp.float32,
            )
            total = part if total is None else total + part
            acc = pv if acc is None else acc + pv
        rows = q_ref.shape[0]
        m_ref[:, lanes] = jnp.broadcast_to(m, (rows, head_dim))
        l_ref[:, lanes] = jnp.broadcast_to(total, (rows, head_dim))
        acc_ref[:, lanes] = acc


def attention_partial(query, pieces):
    tok_rows, width = query.shape
    pairs = width // 128
    in_specs = [pl.BlockSpec((tok_rows, 128), lambda h: (0, h))]
    args = [query]
    for keys, kblk, values, vblk in pieces:
        in_specs.append(pl.BlockSpec((keys.shape[0], 128), lambda h, o=kblk: (0, h + o)))
        in_specs.append(pl.BlockSpec((values.shape[0], 128), lambda h, o=vblk: (0, h + o)))
        args += [keys, values]
    out_spec = pl.BlockSpec((tok_rows, 128), lambda h: (0, h))
    out_shape = jax.ShapeDtypeStruct((tok_rows, width), jnp.float32)
    return pl.pallas_call(
        functools.partial(attn_kernel, n_pieces=len(pieces)),
        grid=(pairs,),
        in_specs=in_specs,
        out_specs=[out_spec] * 3,
        out_shape=[out_shape] * 3,
        compiler_params=pltpu.CompilerParams(vmem_limit_bytes=48 * 1024 * 1024),
    )(*args)


def body(
    hidden_in,
    stale_keys,
    stale_values,
    stale_moments,
    gain_attn,
    bias_attn,
    w_query,
    w_key,
    w_value,
    gain_conv,
    bias_conv,
    conv_weight,
    conv_bias,
    w_time,
    timestep,
):
    devices = lax.axis_size("patch")
    tok_rows = hidden_in.shape[0]
    channels = hidden_in.shape[1]
    all_tokens = tok_rows * devices
    count = all_tokens * (channels // GROUPS)
    ring = YRING
    planes = devices // ring
    half = tok_rows // 2
    vblk = channels // 128

    def perm(dy, dz):
        return [
            (z * ring + y, ((z + dz) % planes) * ring + (y + dy) % ring)
            for z in range(planes)
            for y in range(ring)
        ]

    own_stale = jnp.sum(stale_moments, axis=0)
    stale_all = own_stale
    for flip in range(1, ring):
        if flip & (flip - 1) == 0:
            pairs = [
                (z * ring + y, z * ring + (y ^ flip)) for z in range(planes) for y in range(ring)
            ]
            stale_all = stale_all + lax.ppermute(stale_all, "patch", pairs)
    stale_all = stale_all + lax.ppermute(stale_all, "patch", perm(0, 1))
    kv = jnp.concatenate([stale_keys, stale_values], axis=1)
    from_left = lax.ppermute(kv, "patch", perm(1, 0))
    from_right = lax.ppermute(kv, "patch", perm(-1, 0))
    partner = lax.ppermute(kv, "patch", perm(0, 1))
    far_a = lax.ppermute(from_left[:half], "patch", perm(1, 0))
    far_b = lax.ppermute(from_right[half:], "patch", perm(-1, 0))
    partner_left = lax.ppermute(from_left, "patch", perm(0, 1))
    partner_right = lax.ppermute(partner, "patch", perm(-1, 0))
    partner_far_a = lax.ppermute(partner_left[:half], "patch", perm(1, 0))
    partner_far_b = lax.ppermute(partner_right[half:], "patch", perm(-1, 0))

    total_attn = stale_all[0]
    totals_attn = total_attn - own_stale[0] + group_moments(hidden_in, GROUPS)
    normed = group_normalize(hidden_in, totals_attn, count, gain_attn, bias_attn, GROUPS).astype(
        jnp.bfloat16
    )
    query = jnp.dot(normed, w_query, preferred_element_type=jnp.float32).astype(jnp.bfloat16)
    key_fresh = jnp.dot(normed, w_key, preferred_element_type=jnp.float32).astype(jnp.bfloat16)
    value_fresh = jnp.dot(normed, w_value, preferred_element_type=jnp.float32).astype(jnp.bfloat16)
    query = query * jnp.asarray((channels // HEADS) ** -0.5, jnp.bfloat16)

    far = jnp.concatenate([far_a, far_b], axis=0)
    partner_far = jnp.concatenate([partner_far_a, partner_far_b], axis=0)
    sets = [
        [(key_fresh, 0, value_fresh, 0)]
        + [(a, 0, a, vblk) for a in (from_left, from_right, partner)],
        [(a, 0, a, vblk) for a in (far, partner_left, partner_right)],
        [(partner_far, 0, partner_far, vblk)],
    ]
    partials = []
    for pieces in sets:
        partials.append(attention_partial(query, pieces))
    m = functools.reduce(jnp.maximum, [p[0] for p in partials])
    scales = [jnp.exp(p[0] - m) for p in partials]
    acc = sum(p[2] * r for p, r in zip(partials, scales))
    total = sum(p[1] * r for p, r in zip(partials, scales))
    attended = acc / total
    updated = (hidden_in.astype(jnp.float32) + attended).astype(jnp.bfloat16)
    total_conv = stale_all[1]
    totals_conv = total_conv - own_stale[1] + group_moments(updated, GROUPS)
    normed_conv = group_normalize(updated, totals_conv, count, gain_conv, bias_conv, GROUPS)
    activated = jax.nn.silu(normed_conv).astype(jnp.bfloat16).reshape(tok_rows // W, W, channels)
    rows = activated.shape[0]
    count_p = lax.axis_size("patch")
    top = lax.ppermute(
        activated[rows - 1 :], "patch", [(i, i + 1) for i in range(count_p - 1)]
    )
    bottom = lax.ppermute(activated[:1], "patch", [(i + 1, i) for i in range(count_p - 1)])

    def conv_rows(cells):
        return lax.conv_general_dilated(
            cells[None],
            conv_weight,
            (1, 1),
            ((0, 0), (1, 1)),
            dimension_numbers=("NHWC", "HWIO", "NHWC"),
            preferred_element_type=jnp.float32,
        )[0]

    inner = conv_rows(activated)
    first_row = conv_rows(jnp.concatenate([top, activated[:2]], axis=0))
    last_row = conv_rows(jnp.concatenate([activated[rows - 2 :], bottom], axis=0))
    convolved = jnp.concatenate([first_row, inner, last_row], axis=0)
    temb = time_embedding(timestep, w_time)
    conv_out = (convolved + conv_bias + temb).astype(jnp.bfloat16)
    return conv_out.reshape(tok_rows, conv_weight.shape[3])


def solution(mesh):
    return jax.shard_map(
        body,
        mesh=mesh,
        in_specs=(
            P(("batch", "patch"), None),
            P(("batch", "patch"), None),
            P(("batch", "patch"), None),
            P(("batch", "patch"), None, None, None),
            P(),
            P(),
            P(),
            P(),
            P(),
            P(),
            P(),
            P(),
            P(),
            P(),
            P(),
        ),
        out_specs=P(("batch", "patch"), None),
        check_vma=False,
    )
```

```python
import functools
import math

import jax
import jax.numpy as jnp
from jax import lax
from jax.sharding import PartitionSpec as P
from jax.experimental import pallas as pl
from jax.experimental.pallas import tpu as pltpu

HEADS = 20
GROUPS = 32
W = 64
HEAD_DIM = 64
YRING = 4


EPS = 1e-05


def group_moments(rows_in, groups):
    values = rows_in.astype(jnp.float32).reshape(
        rows_in.shape[0], groups, rows_in.shape[1] // groups
    )
    return jnp.stack([jnp.sum(values, axis=(0, 2)), jnp.sum(values * values, axis=(0, 2))])


def group_normalize(rows_in, totals, count, gain, offset, groups):
    average = totals[0] / count
    variance = totals[1] / count - average * average
    inverse = lax.rsqrt(variance + EPS)
    group_width = rows_in.shape[1] // groups
    factors = jnp.repeat(inverse, group_width) * gain
    shifts = offset - jnp.repeat(average * inverse, group_width) * gain
    return rows_in.astype(jnp.float32) * factors + shifts


def time_embedding(timestep, w_time):
    half_dim = w_time.shape[0] // 2
    frequency = jnp.exp(-math.log(10000.0) * jnp.arange(half_dim, dtype=jnp.float32) / half_dim)
    angles = timestep[0].astype(jnp.float32) * frequency
    embedded = jnp.concatenate([jnp.cos(angles), jnp.sin(angles)])
    return jnp.dot(embedded[None, :], w_time.astype(jnp.float32), precision=lax.Precision.HIGHEST)[
        0
    ]


def attn_kernel(*refs, n_pieces, carry, final):
    q_ref = refs[0]
    pos = 1
    if carry:
        mp_ref, lp_ref, accp_ref = refs[pos : pos + 3]
        pos += 3
    if final:
        h_ref = refs[pos]
        pos += 1
    piece_refs = refs[pos : pos + 2 * n_pieces]
    out_refs = refs[pos + 2 * n_pieces :]
    head_dim = HEAD_DIM
    rows = q_ref.shape[0]
    dims = (((1,), (1,)), ((), ()))
    for hh in range(q_ref.shape[1] // head_dim):
        lanes = slice(hh * head_dim, (hh + 1) * head_dim)
        qh = q_ref[:, lanes]
        scores = [
            lax.dot_general(
                qh, piece_refs[2 * i][:, lanes], dims, preferred_element_type=jnp.float32
            )
            for i in range(n_pieces)
        ]
        m = functools.reduce(jnp.maximum, [jnp.max(s, axis=1, keepdims=True) for s in scores])
        if carry:
            m_prev = jnp.max(mp_ref[:, lanes], axis=1, keepdims=True)
            m = jnp.maximum(m, m_prev)
            rescale = jnp.exp(m_prev - m)
            total = jnp.max(lp_ref[:, lanes], axis=1, keepdims=True) * rescale
            acc = accp_ref[:, lanes] * rescale
        else:
            total = None
            acc = None
        for i in range(n_pieces):
            w = jnp.exp(scores[i] - m)
            part = jnp.sum(w, axis=1, keepdims=True)
            pv = jnp.dot(
                w.astype(jnp.bfloat16),
                piece_refs[2 * i + 1][:, lanes],
                preferred_element_type=jnp.float32,
            )
            total = part if total is None else total + part
            acc = pv if acc is None else acc + pv
        if final:
            (o_ref,) = out_refs
            o_ref[:, lanes] = (h_ref[:, lanes].astype(jnp.float32) + acc / total).astype(
                jnp.bfloat16
            )
        else:
            m_ref, l_ref, acc_ref = out_refs
            m_ref[:, lanes] = jnp.broadcast_to(m, (rows, head_dim))
            l_ref[:, lanes] = jnp.broadcast_to(total, (rows, head_dim))
            acc_ref[:, lanes] = acc


def attention_partial(query, pieces, carry=None, hidden=None, block=128):
    tok_rows, width = query.shape
    steps = width // block
    in_specs = [pl.BlockSpec((tok_rows, block), lambda h: (0, h))]
    args = [query]
    if carry is not None:
        in_specs += [pl.BlockSpec((tok_rows, block), lambda h: (0, h))] * 3
        args += list(carry)
    if hidden is not None:
        in_specs.append(pl.BlockSpec((tok_rows, block), lambda h: (0, h)))
        args.append(hidden)
    for keys, kblk, values, vblk in pieces:
        ko = kblk * 128 // block
        vo = vblk * 128 // block
        in_specs.append(pl.BlockSpec((keys.shape[0], block), lambda h, o=ko: (0, h + o)))
        in_specs.append(pl.BlockSpec((values.shape[0], block), lambda h, o=vo: (0, h + o)))
        args += [keys, values]
    out_spec = pl.BlockSpec((tok_rows, block), lambda h: (0, h))
    if hidden is not None:
        out_specs = out_spec
        out_shape = jax.ShapeDtypeStruct((tok_rows, width), jnp.bfloat16)
    else:
        out_specs = [out_spec] * 3
        out_shape = [jax.ShapeDtypeStruct((tok_rows, width), jnp.float32)] * 3
    return pl.pallas_call(
        functools.partial(
            attn_kernel,
            n_pieces=len(pieces),
            carry=carry is not None,
            final=hidden is not None,
        ),
        grid=(steps,),
        in_specs=in_specs,
        out_specs=out_specs,
        out_shape=out_shape,
        compiler_params=pltpu.CompilerParams(vmem_limit_bytes=48 * 1024 * 1024),
    )(*args)


def body(
    hidden_in,
    stale_keys,
    stale_values,
    stale_moments,
    gain_attn,
    bias_attn,
    w_query,
    w_key,
    w_value,
    gain_conv,
    bias_conv,
    conv_weight,
    conv_bias,
    w_time,
    timestep,
):
    devices = lax.axis_size("patch")
    tok_rows = hidden_in.shape[0]
    channels = hidden_in.shape[1]
    all_tokens = tok_rows * devices
    count = all_tokens * (channels // GROUPS)
    ring = YRING
    planes = devices // ring
    half = tok_rows // 2
    vblk = channels // 128

    def perm(dy, dz):
        return [
            (z * ring + y, ((z + dz) % planes) * ring + (y + dy) % ring)
            for z in range(planes)
            for y in range(ring)
        ]

    own_stale = jnp.sum(stale_moments, axis=0)
    stale_all = own_stale
    for flip in range(1, ring):
        if flip & (flip - 1) == 0:
            pairs = [
                (z * ring + y, z * ring + (y ^ flip)) for z in range(planes) for y in range(ring)
            ]
            stale_all = stale_all + lax.ppermute(stale_all, "patch", pairs)
    stale_all = stale_all + lax.ppermute(stale_all, "patch", perm(0, 1))
    kv = jnp.concatenate([stale_keys, stale_values], axis=1)
    from_left = lax.ppermute(kv, "patch", perm(1, 0))
    from_right = lax.ppermute(kv, "patch", perm(-1, 0))
    partner = lax.ppermute(kv, "patch", perm(0, 1))
    far_a = lax.ppermute(from_left[:half], "patch", perm(1, 0))
    far_b = lax.ppermute(from_right[half:], "patch", perm(-1, 0))
    partner_left = lax.ppermute(from_left, "patch", perm(0, 1))
    partner_right = lax.ppermute(partner, "patch", perm(-1, 0))
    partner_far_a = lax.ppermute(partner_left[:half], "patch", perm(1, 0))
    partner_far_b = lax.ppermute(partner_right[half:], "patch", perm(-1, 0))

    total_attn = stale_all[0]
    totals_attn = total_attn - own_stale[0] + group_moments(hidden_in, GROUPS)
    normed = group_normalize(hidden_in, totals_attn, count, gain_attn, bias_attn, GROUPS).astype(
        jnp.bfloat16
    )
    query = jnp.dot(normed, w_query, preferred_element_type=jnp.float32).astype(jnp.bfloat16)
    key_fresh = jnp.dot(normed, w_key, preferred_element_type=jnp.float32).astype(jnp.bfloat16)
    value_fresh = jnp.dot(normed, w_value, preferred_element_type=jnp.float32).astype(jnp.bfloat16)
    query = query * jnp.asarray((channels // HEADS) ** -0.5, jnp.bfloat16)

    far = jnp.concatenate([far_a, far_b], axis=0)
    partner_far = jnp.concatenate([partner_far_a, partner_far_b], axis=0)
    sets = [
        [(key_fresh, 0, value_fresh, 0)]
        + [(a, 0, a, vblk) for a in (from_left, from_right, partner)],
        [(a, 0, a, vblk) for a in (far, partner_left, partner_right)],
        [(partner_far, 0, partner_far, vblk)],
    ]
    state = attention_partial(query, sets[0])
    state = attention_partial(query, sets[1], carry=state)
    updated = attention_partial(query, sets[2], carry=state, hidden=hidden_in, block=256)
    total_conv = stale_all[1]
    totals_conv = total_conv - own_stale[1] + group_moments(updated, GROUPS)
    normed_conv = group_normalize(updated, totals_conv, count, gain_conv, bias_conv, GROUPS)
    activated = jax.nn.silu(normed_conv).astype(jnp.bfloat16).reshape(tok_rows // W, W, channels)
    rows = activated.shape[0]
    count_p = lax.axis_size("patch")
    top = lax.ppermute(
        activated[rows - 1 :], "patch", [(i, i + 1) for i in range(count_p - 1)]
    )
    bottom = lax.ppermute(activated[:1], "patch", [(i + 1, i) for i in range(count_p - 1)])

    def conv_rows(cells):
        return lax.conv_general_dilated(
            cells[None],
            conv_weight,
            (1, 1),
            ((0, 0), (1, 1)),
            dimension_numbers=("NHWC", "HWIO", "NHWC"),
            preferred_element_type=jnp.float32,
        )[0]

    inner = conv_rows(activated)
    first_row = conv_rows(jnp.concatenate([top, activated[:2]], axis=0))
    last_row = conv_rows(jnp.concatenate([activated[rows - 2 :], bottom], axis=0))
    convolved = jnp.concatenate([first_row, inner, last_row], axis=0)
    temb = time_embedding(timestep, w_time)
    conv_out = (convolved + conv_bias + temb).astype(jnp.bfloat16)
    return conv_out.reshape(tok_rows, conv_weight.shape[3])


def solution(mesh):
    return jax.shard_map(
        body,
        mesh=mesh,
        in_specs=(
            P(("batch", "patch"), None),
            P(("batch", "patch"), None),
            P(("batch", "patch"), None),
            P(("batch", "patch"), None, None, None),
            P(),
            P(),
            P(),
            P(),
            P(),
            P(),
            P(),
            P(),
            P(),
            P(),
            P(),
        ),
        out_specs=P(("batch", "patch"), None),
        check_vma=False,
    )
```

```python
import functools
import math

import jax
import jax.numpy as jnp
from jax import lax
from jax.sharding import PartitionSpec as P
from jax.experimental import pallas as pl
from jax.experimental.pallas import tpu as pltpu

HEADS = 20
GROUPS = 32
W = 64
HEAD_DIM = 64
YRING = 4


EPS = 1e-05


def group_moments(rows_in, groups):
    values = rows_in.astype(jnp.float32).reshape(
        rows_in.shape[0], groups, rows_in.shape[1] // groups
    )
    return jnp.stack([jnp.sum(values, axis=(0, 2)), jnp.sum(values * values, axis=(0, 2))])


def group_normalize(rows_in, totals, count, gain, offset, groups):
    average = totals[0] / count
    variance = totals[1] / count - average * average
    inverse = lax.rsqrt(variance + EPS)
    group_width = rows_in.shape[1] // groups
    factors = jnp.repeat(inverse, group_width) * gain
    shifts = offset - jnp.repeat(average * inverse, group_width) * gain
    return rows_in.astype(jnp.float32) * factors + shifts


def time_embedding(timestep, w_time):
    half_dim = w_time.shape[0] // 2
    frequency = jnp.exp(-math.log(10000.0) * jnp.arange(half_dim, dtype=jnp.float32) / half_dim)
    angles = timestep[0].astype(jnp.float32) * frequency
    embedded = jnp.concatenate([jnp.cos(angles), jnp.sin(angles)])
    return jnp.dot(embedded[None, :], w_time.astype(jnp.float32), precision=lax.Precision.HIGHEST)[
        0
    ]


def attn_kernel(*refs, n_pieces):
    q_ref = refs[0]
    piece_refs = refs[1 : 1 + 2 * n_pieces]
    m_ref, l_ref, acc_ref = refs[1 + 2 * n_pieces :]
    head_dim = HEAD_DIM
    dims = (((1,), (1,)), ((), ()))
    for hh in range(q_ref.shape[1] // head_dim):
        lanes = slice(hh * head_dim, (hh + 1) * head_dim)
        qh = q_ref[:, lanes]
        scores = [
            lax.dot_general(
                qh, piece_refs[2 * i][:, lanes], dims, preferred_element_type=jnp.float32
            )
            for i in range(n_pieces)
        ]
        m = functools.reduce(jnp.maximum, [jnp.max(s, axis=1, keepdims=True) for s in scores])
        total = None
        acc = None
        for i in range(n_pieces):
            w = jnp.exp(scores[i] - m)
            part = jnp.sum(w, axis=1, keepdims=True)
            pv = jnp.dot(
                w.astype(jnp.bfloat16),
                piece_refs[2 * i + 1][:, lanes],
                preferred_element_type=jnp.float32,
            )
            total = part if total is None else total + part
            acc = pv if acc is None else acc + pv
        rows = q_ref.shape[0]
        m_ref[:, lanes] = jnp.broadcast_to(m, (rows, head_dim))
        l_ref[:, lanes] = jnp.broadcast_to(total, (rows, head_dim))
        acc_ref[:, lanes] = acc


def attention_partial(query, pieces, block=128):
    tok_rows, width = query.shape
    pairs = width // block
    in_specs = [pl.BlockSpec((tok_rows, block), lambda h: (0, h))]
    args = [query]
    for keys, kblk, values, vblk in pieces:
        ko = kblk * 128 // block
        vo = vblk * 128 // block
        in_specs.append(pl.BlockSpec((keys.shape[0], block), lambda h, o=ko: (0, h + o)))
        in_specs.append(pl.BlockSpec((values.shape[0], block), lambda h, o=vo: (0, h + o)))
        args += [keys, values]
    out_spec = pl.BlockSpec((tok_rows, block), lambda h: (0, h))
    out_shape = jax.ShapeDtypeStruct((tok_rows, width), jnp.float32)
    return pl.pallas_call(
        functools.partial(attn_kernel, n_pieces=len(pieces)),
        grid=(pairs,),
        in_specs=in_specs,
        out_specs=[out_spec] * 3,
        out_shape=[out_shape] * 3,
        compiler_params=pltpu.CompilerParams(vmem_limit_bytes=48 * 1024 * 1024),
    )(*args)


def body(
    hidden_in,
    stale_keys,
    stale_values,
    stale_moments,
    gain_attn,
    bias_attn,
    w_query,
    w_key,
    w_value,
    gain_conv,
    bias_conv,
    conv_weight,
    conv_bias,
    w_time,
    timestep,
):
    devices = lax.axis_size("patch")
    tok_rows = hidden_in.shape[0]
    channels = hidden_in.shape[1]
    all_tokens = tok_rows * devices
    count = all_tokens * (channels // GROUPS)
    ring = YRING
    planes = devices // ring
    half = tok_rows // 2
    vblk = channels // 128

    def perm(dy, dz):
        return [
            (z * ring + y, ((z + dz) % planes) * ring + (y + dy) % ring)
            for z in range(planes)
            for y in range(ring)
        ]

    own_stale = jnp.sum(stale_moments, axis=0)
    stale_all = own_stale
    for flip in range(1, ring):
        if flip & (flip - 1) == 0:
            pairs = [
                (z * ring + y, z * ring + (y ^ flip)) for z in range(planes) for y in range(ring)
            ]
            stale_all = stale_all + lax.ppermute(stale_all, "patch", pairs)
    stale_all = stale_all + lax.ppermute(stale_all, "patch", perm(0, 1))
    kv = jnp.concatenate([stale_keys, stale_values], axis=1)
    from_left = lax.ppermute(kv, "patch", perm(1, 0))
    from_right = lax.ppermute(kv, "patch", perm(-1, 0))
    partner = lax.ppermute(kv, "patch", perm(0, 1))
    far = lax.ppermute(from_left, "patch", perm(1, 0))
    partner_left = lax.ppermute(from_left, "patch", perm(0, 1))
    partner_right = lax.ppermute(partner, "patch", perm(-1, 0))
    partner_far_a = lax.ppermute(partner_left[:half], "patch", perm(1, 0))
    partner_far_b = lax.ppermute(partner_right[half:], "patch", perm(-1, 0))

    total_attn = stale_all[0]
    totals_attn = total_attn - own_stale[0] + group_moments(hidden_in, GROUPS)
    normed = group_normalize(hidden_in, totals_attn, count, gain_attn, bias_attn, GROUPS).astype(
        jnp.bfloat16
    )
    query = jnp.dot(normed, w_query, preferred_element_type=jnp.float32).astype(jnp.bfloat16)
    key_fresh = jnp.dot(normed, w_key, preferred_element_type=jnp.float32).astype(jnp.bfloat16)
    value_fresh = jnp.dot(normed, w_value, preferred_element_type=jnp.float32).astype(jnp.bfloat16)
    query = query * jnp.asarray((channels // HEADS) ** -0.5, jnp.bfloat16)

    partner_far = jnp.concatenate([partner_far_a, partner_far_b], axis=0)
    sets = [
        [(key_fresh, 0, value_fresh, 0)]
        + [(a, 0, a, vblk) for a in (from_left, from_right, partner)],
        [(a, 0, a, vblk) for a in (far, partner_left, partner_right)],
        [(partner_far, 0, partner_far, vblk)],
    ]
    partials = []
    for i, pieces in enumerate(sets):
        partials.append(attention_partial(query, pieces, block=256 if i == 2 else 128))
    m = functools.reduce(jnp.maximum, [p[0] for p in partials])
    scales = [jnp.exp(p[0] - m) for p in partials]
    acc = sum(p[2] * r for p, r in zip(partials, scales))
    total = sum(p[1] * r for p, r in zip(partials, scales))
    attended = acc / total
    updated = (hidden_in.astype(jnp.float32) + attended).astype(jnp.bfloat16)
    total_conv = stale_all[1]
    totals_conv = total_conv - own_stale[1] + group_moments(updated, GROUPS)
    normed_conv = group_normalize(updated, totals_conv, count, gain_conv, bias_conv, GROUPS)
    activated = jax.nn.silu(normed_conv).astype(jnp.bfloat16).reshape(tok_rows // W, W, channels)
    rows = activated.shape[0]
    count_p = lax.axis_size("patch")
    top = lax.ppermute(
        activated[rows - 1 :], "patch", [(i, i + 1) for i in range(count_p - 1)]
    )
    bottom = lax.ppermute(activated[:1], "patch", [(i + 1, i) for i in range(count_p - 1)])

    def conv_rows(cells):
        return lax.conv_general_dilated(
            cells,
            conv_weight,
            (1, 1),
            ((0, 0), (1, 1)),
            dimension_numbers=("NHWC", "HWIO", "NHWC"),
            preferred_element_type=jnp.float32,
        )

    inner = conv_rows(activated[None])[0]
    edges = conv_rows(
        jnp.stack(
            [
                jnp.concatenate([top, activated[:2]], axis=0),
                jnp.concatenate([activated[rows - 2 :], bottom], axis=0),
            ]
        )
    )
    convolved = jnp.concatenate([edges[0], inner, edges[1]], axis=0)
    temb = time_embedding(timestep, w_time)
    conv_out = (convolved + conv_bias + temb).astype(jnp.bfloat16)
    return conv_out.reshape(tok_rows, conv_weight.shape[3])


def solution(mesh):
    return jax.shard_map(
        body,
        mesh=mesh,
        in_specs=(
            P(("batch", "patch"), None),
            P(("batch", "patch"), None),
            P(("batch", "patch"), None),
            P(("batch", "patch"), None, None, None),
            P(),
            P(),
            P(),
            P(),
            P(),
            P(),
            P(),
            P(),
            P(),
            P(),
            P(),
        ),
        out_specs=P(("batch", "patch"), None),
        check_vma=False,
    )
```

```python
import functools
import math

import jax
import jax.numpy as jnp
from jax import lax
from jax.sharding import PartitionSpec as P
from jax.experimental import pallas as pl
from jax.experimental.pallas import tpu as pltpu

HEADS = 20
GROUPS = 32
W = 64
HEAD_DIM = 64
YRING = 4


EPS = 1e-05


def group_moments(rows_in, groups):
    values = rows_in.astype(jnp.float32).reshape(
        rows_in.shape[0], groups, rows_in.shape[1] // groups
    )
    return jnp.stack([jnp.sum(values, axis=(0, 2)), jnp.sum(values * values, axis=(0, 2))])


def group_normalize(rows_in, totals, count, gain, offset, groups):
    average = totals[0] / count
    variance = totals[1] / count - average * average
    inverse = lax.rsqrt(variance + EPS)
    group_width = rows_in.shape[1] // groups
    factors = jnp.repeat(inverse, group_width) * gain
    shifts = offset - jnp.repeat(average * inverse, group_width) * gain
    return rows_in.astype(jnp.float32) * factors + shifts


def time_embedding(timestep, w_time):
    half_dim = w_time.shape[0] // 2
    frequency = jnp.exp(-math.log(10000.0) * jnp.arange(half_dim, dtype=jnp.float32) / half_dim)
    angles = timestep[0].astype(jnp.float32) * frequency
    embedded = jnp.concatenate([jnp.cos(angles), jnp.sin(angles)])
    return jnp.dot(embedded[None, :], w_time.astype(jnp.float32), precision=lax.Precision.HIGHEST)[
        0
    ]


def attn_kernel(*refs, n_pieces):
    q_ref = refs[0]
    piece_refs = refs[1 : 1 + 2 * n_pieces]
    m_ref, l_ref, acc_ref = refs[1 + 2 * n_pieces :]
    head_dim = HEAD_DIM
    dims = (((1,), (1,)), ((), ()))
    for hh in range(q_ref.shape[1] // head_dim):
        lanes = slice(hh * head_dim, (hh + 1) * head_dim)
        qh = q_ref[:, lanes]
        scores = [
            lax.dot_general(
                qh, piece_refs[2 * i][:, lanes], dims, preferred_element_type=jnp.float32
            )
            for i in range(n_pieces)
        ]
        m = functools.reduce(jnp.maximum, [jnp.max(s, axis=1, keepdims=True) for s in scores])
        total = None
        acc = None
        for i in range(n_pieces):
            w = jnp.exp(scores[i] - m)
            part = jnp.sum(w, axis=1, keepdims=True)
            pv = jnp.dot(
                w.astype(jnp.bfloat16),
                piece_refs[2 * i + 1][:, lanes],
                preferred_element_type=jnp.float32,
            )
            total = part if total is None else total + part
            acc = pv if acc is None else acc + pv
        rows = q_ref.shape[0]
        m_ref[:, lanes] = jnp.broadcast_to(m, (rows, head_dim))
        l_ref[:, lanes] = jnp.broadcast_to(total, (rows, head_dim))
        acc_ref[:, lanes] = acc


def attention_partial(query, pieces, block=128):
    tok_rows, width = query.shape
    pairs = width // block
    in_specs = [pl.BlockSpec((tok_rows, block), lambda h: (0, h))]
    args = [query]
    for keys, kblk, values, vblk in pieces:
        ko = kblk * 128 // block
        vo = vblk * 128 // block
        in_specs.append(pl.BlockSpec((keys.shape[0], block), lambda h, o=ko: (0, h + o)))
        in_specs.append(pl.BlockSpec((values.shape[0], block), lambda h, o=vo: (0, h + o)))
        args += [keys, values]
    out_spec = pl.BlockSpec((tok_rows, block), lambda h: (0, h))
    out_shape = jax.ShapeDtypeStruct((tok_rows, width), jnp.float32)
    return pl.pallas_call(
        functools.partial(attn_kernel, n_pieces=len(pieces)),
        grid=(pairs,),
        in_specs=in_specs,
        out_specs=[out_spec] * 3,
        out_shape=[out_shape] * 3,
        compiler_params=pltpu.CompilerParams(vmem_limit_bytes=48 * 1024 * 1024),
    )(*args)


def body(
    hidden_in,
    stale_keys,
    stale_values,
    stale_moments,
    gain_attn,
    bias_attn,
    w_query,
    w_key,
    w_value,
    gain_conv,
    bias_conv,
    conv_weight,
    conv_bias,
    w_time,
    timestep,
):
    devices = lax.axis_size("patch")
    tok_rows = hidden_in.shape[0]
    channels = hidden_in.shape[1]
    all_tokens = tok_rows * devices
    count = all_tokens * (channels // GROUPS)
    ring = YRING
    planes = devices // ring
    half = tok_rows // 2
    tail_cut = 2 * tok_rows // 3
    vblk = channels // 128

    def perm(dy, dz):
        return [
            (z * ring + y, ((z + dz) % planes) * ring + (y + dy) % ring)
            for z in range(planes)
            for y in range(ring)
        ]

    own_stale = jnp.sum(stale_moments, axis=0)
    stale_all = own_stale
    for flip in range(1, ring):
        if flip & (flip - 1) == 0:
            pairs = [
                (z * ring + y, z * ring + (y ^ flip)) for z in range(planes) for y in range(ring)
            ]
            stale_all = stale_all + lax.ppermute(stale_all, "patch", pairs)
    stale_all = stale_all + lax.ppermute(stale_all, "patch", perm(0, 1))
    kv = jnp.concatenate([stale_keys, stale_values], axis=1)
    from_left = lax.ppermute(kv, "patch", perm(1, 0))
    from_right = lax.ppermute(kv, "patch", perm(-1, 0))
    partner = lax.ppermute(kv, "patch", perm(0, 1))
    far_a = lax.ppermute(from_left[:half], "patch", perm(1, 0))
    far_b = lax.ppermute(from_right[half:], "patch", perm(-1, 0))
    partner_left = lax.ppermute(from_left, "patch", perm(0, 1))
    partner_right = lax.ppermute(partner, "patch", perm(-1, 0))
    partner_far_a = lax.ppermute(partner_left[:tail_cut], "patch", perm(1, 0))
    partner_far_b = lax.ppermute(partner_right[tail_cut:], "patch", perm(-1, 0))

    total_attn = stale_all[0]
    totals_attn = total_attn - own_stale[0] + group_moments(hidden_in, GROUPS)
    normed = group_normalize(hidden_in, totals_attn, count, gain_attn, bias_attn, GROUPS).astype(
        jnp.bfloat16
    )
    query = jnp.dot(normed, w_query, preferred_element_type=jnp.float32).astype(jnp.bfloat16)
    key_fresh = jnp.dot(normed, w_key, preferred_element_type=jnp.float32).astype(jnp.bfloat16)
    value_fresh = jnp.dot(normed, w_value, preferred_element_type=jnp.float32).astype(jnp.bfloat16)
    query = query * jnp.asarray((channels // HEADS) ** -0.5, jnp.bfloat16)

    far = jnp.concatenate([far_a, far_b], axis=0)
    partner_far = jnp.concatenate([partner_far_a, partner_far_b], axis=0)
    sets = [
        [(key_fresh, 0, value_fresh, 0)]
        + [(a, 0, a, vblk) for a in (from_left, from_right, partner)],
        [(a, 0, a, vblk) for a in (far, partner_left, partner_right)],
        [(partner_far, 0, partner_far, vblk)],
    ]
    partials = []
    for i, pieces in enumerate(sets):
        partials.append(attention_partial(query, pieces, block=256 if i == 2 else 128))
    m = functools.reduce(jnp.maximum, [p[0] for p in partials])
    scales = [jnp.exp(p[0] - m) for p in partials]
    acc = sum(p[2] * r for p, r in zip(partials, scales))
    total = sum(p[1] * r for p, r in zip(partials, scales))
    attended = acc / total
    updated = (hidden_in.astype(jnp.float32) + attended).astype(jnp.bfloat16)
    total_conv = stale_all[1]
    totals_conv = total_conv - own_stale[1] + group_moments(updated, GROUPS)
    normed_conv = group_normalize(updated, totals_conv, count, gain_conv, bias_conv, GROUPS)
    activated = jax.nn.silu(normed_conv).astype(jnp.bfloat16).reshape(tok_rows // W, W, channels)
    rows = activated.shape[0]
    count_p = lax.axis_size("patch")
    top = lax.ppermute(
        activated[rows - 1 :], "patch", [(i, i + 1) for i in range(count_p - 1)]
    )
    bottom = lax.ppermute(activated[:1], "patch", [(i + 1, i) for i in range(count_p - 1)])

    def conv_rows(cells):
        return lax.conv_general_dilated(
            cells,
            conv_weight,
            (1, 1),
            ((0, 0), (1, 1)),
            dimension_numbers=("NHWC", "HWIO", "NHWC"),
            preferred_element_type=jnp.float32,
        )

    inner = conv_rows(activated[None])[0]
    edges = conv_rows(
        jnp.stack(
            [
                jnp.concatenate([top, activated[:2]], axis=0),
                jnp.concatenate([activated[rows - 2 :], bottom], axis=0),
            ]
        )
    )
    convolved = jnp.concatenate([edges[0], inner, edges[1]], axis=0)
    temb = time_embedding(timestep, w_time)
    conv_out = (convolved + conv_bias + temb).astype(jnp.bfloat16)
    return conv_out.reshape(tok_rows, conv_weight.shape[3])


def solution(mesh):
    return jax.shard_map(
        body,
        mesh=mesh,
        in_specs=(
            P(("batch", "patch"), None),
            P(("batch", "patch"), None),
            P(("batch", "patch"), None),
            P(("batch", "patch"), None, None, None),
            P(),
            P(),
            P(),
            P(),
            P(),
            P(),
            P(),
            P(),
            P(),
            P(),
            P(),
        ),
        out_specs=P(("batch", "patch"), None),
        check_vma=False,
    )
```

```python
import functools
import math

import jax
import jax.numpy as jnp
from jax import lax
from jax.sharding import PartitionSpec as P
from jax.experimental import pallas as pl
from jax.experimental.pallas import tpu as pltpu

HEADS = 20
GROUPS = 32
W = 64
HEAD_DIM = 64
BLOCKS = (128, 1280, 256)
YRING = 4


EPS = 1e-05


def group_moments(rows_in, groups):
    values = rows_in.astype(jnp.float32).reshape(
        rows_in.shape[0], groups, rows_in.shape[1] // groups
    )
    return jnp.stack([jnp.sum(values, axis=(0, 2)), jnp.sum(values * values, axis=(0, 2))])


def group_normalize(rows_in, totals, count, gain, offset, groups):
    average = totals[0] / count
    variance = totals[1] / count - average * average
    inverse = lax.rsqrt(variance + EPS)
    group_width = rows_in.shape[1] // groups
    factors = jnp.repeat(inverse, group_width) * gain
    shifts = offset - jnp.repeat(average * inverse, group_width) * gain
    return rows_in.astype(jnp.float32) * factors + shifts


def time_embedding(timestep, w_time):
    half_dim = w_time.shape[0] // 2
    frequency = jnp.exp(-math.log(10000.0) * jnp.arange(half_dim, dtype=jnp.float32) / half_dim)
    angles = timestep[0].astype(jnp.float32) * frequency
    embedded = jnp.concatenate([jnp.cos(angles), jnp.sin(angles)])
    return jnp.dot(embedded[None, :], w_time.astype(jnp.float32), precision=lax.Precision.HIGHEST)[
        0
    ]


def attn_kernel(*refs, n_pieces):
    q_ref = refs[0]
    piece_refs = refs[1 : 1 + 2 * n_pieces]
    m_ref, l_ref, acc_ref = refs[1 + 2 * n_pieces :]
    head_dim = HEAD_DIM
    dims = (((1,), (1,)), ((), ()))
    for hh in range(q_ref.shape[1] // head_dim):
        lanes = slice(hh * head_dim, (hh + 1) * head_dim)
        qh = q_ref[:, lanes]
        scores = [
            lax.dot_general(
                qh, piece_refs[2 * i][:, lanes], dims, preferred_element_type=jnp.float32
            )
            for i in range(n_pieces)
        ]
        m = functools.reduce(jnp.maximum, [jnp.max(s, axis=1, keepdims=True) for s in scores])
        total = None
        acc = None
        for i in range(n_pieces):
            w = jnp.exp(scores[i] - m)
            part = jnp.sum(w, axis=1, keepdims=True)
            pv = jnp.dot(
                w.astype(jnp.bfloat16),
                piece_refs[2 * i + 1][:, lanes],
                preferred_element_type=jnp.float32,
            )
            total = part if total is None else total + part
            acc = pv if acc is None else acc + pv
        rows = q_ref.shape[0]
        m_ref[:, lanes] = jnp.broadcast_to(m, (rows, head_dim))
        l_ref[:, lanes] = jnp.broadcast_to(total, (rows, head_dim))
        acc_ref[:, lanes] = acc


def attention_partial(query, pieces, block=128):
    tok_rows, width = query.shape
    pairs = width // block
    in_specs = [pl.BlockSpec((tok_rows, block), lambda h: (0, h))]
    args = [query]
    for keys, kblk, values, vblk in pieces:
        ko = kblk * 128 // block
        vo = vblk * 128 // block
        in_specs.append(pl.BlockSpec((keys.shape[0], block), lambda h, o=ko: (0, h + o)))
        in_specs.append(pl.BlockSpec((values.shape[0], block), lambda h, o=vo: (0, h + o)))
        args += [keys, values]
    out_spec = pl.BlockSpec((tok_rows, block), lambda h: (0, h))
    out_shape = jax.ShapeDtypeStruct((tok_rows, width), jnp.float32)
    return pl.pallas_call(
        functools.partial(attn_kernel, n_pieces=len(pieces)),
        grid=(pairs,),
        in_specs=in_specs,
        out_specs=[out_spec] * 3,
        out_shape=[out_shape] * 3,
        compiler_params=pltpu.CompilerParams(vmem_limit_bytes=48 * 1024 * 1024),
    )(*args)


def body(
    hidden_in,
    stale_keys,
    stale_values,
    stale_moments,
    gain_attn,
    bias_attn,
    w_query,
    w_key,
    w_value,
    gain_conv,
    bias_conv,
    conv_weight,
    conv_bias,
    w_time,
    timestep,
):
    devices = lax.axis_size("patch")
    tok_rows = hidden_in.shape[0]
    channels = hidden_in.shape[1]
    all_tokens = tok_rows * devices
    count = all_tokens * (channels // GROUPS)
    ring = YRING
    planes = devices // ring
    half = tok_rows // 2
    vblk = channels // 128

    def perm(dy, dz):
        return [
            (z * ring + y, ((z + dz) % planes) * ring + (y + dy) % ring)
            for z in range(planes)
            for y in range(ring)
        ]

    own_stale = jnp.sum(stale_moments, axis=0)
    stale_all = own_stale
    for flip in range(1, ring):
        if flip & (flip - 1) == 0:
            pairs = [
                (z * ring + y, z * ring + (y ^ flip)) for z in range(planes) for y in range(ring)
            ]
            stale_all = stale_all + lax.ppermute(stale_all, "patch", pairs)
    stale_all = stale_all + lax.ppermute(stale_all, "patch", perm(0, 1))
    kv = jnp.concatenate([stale_keys, stale_values], axis=1)
    from_left = lax.ppermute(kv, "patch", perm(1, 0))
    from_right = lax.ppermute(kv, "patch", perm(-1, 0))
    partner = lax.ppermute(kv, "patch", perm(0, 1))
    far_a = lax.ppermute(from_left[:half], "patch", perm(1, 0))
    far_b = lax.ppermute(from_right[half:], "patch", perm(-1, 0))
    partner_left = lax.ppermute(from_left, "patch", perm(0, 1))
    partner_right = lax.ppermute(partner, "patch", perm(-1, 0))
    partner_far_a = lax.ppermute(partner_left[:half], "patch", perm(1, 0))
    partner_far_b = lax.ppermute(partner_right[half:], "patch", perm(-1, 0))

    total_attn = stale_all[0]
    totals_attn = total_attn - own_stale[0] + group_moments(hidden_in, GROUPS)
    normed = group_normalize(hidden_in, totals_attn, count, gain_attn, bias_attn, GROUPS).astype(
        jnp.bfloat16
    )
    query = jnp.dot(normed, w_query, preferred_element_type=jnp.float32).astype(jnp.bfloat16)
    key_fresh = jnp.dot(normed, w_key, preferred_element_type=jnp.float32).astype(jnp.bfloat16)
    value_fresh = jnp.dot(normed, w_value, preferred_element_type=jnp.float32).astype(jnp.bfloat16)
    query = query * jnp.asarray((channels // HEADS) ** -0.5, jnp.bfloat16)

    far = jnp.concatenate([far_a, far_b], axis=0)
    partner_far = jnp.concatenate([partner_far_a, partner_far_b], axis=0)
    sets = [
        [(key_fresh, 0, value_fresh, 0)]
        + [(a, 0, a, vblk) for a in (from_left, from_right, partner)],
        [(a, 0, a, vblk) for a in (far, partner_left, partner_right)],
        [(partner_far, 0, partner_far, vblk)],
    ]
    partials = []
    for i, pieces in enumerate(sets):
        partials.append(attention_partial(query, pieces, block=BLOCKS[i]))
    m = functools.reduce(jnp.maximum, [p[0] for p in partials])
    scales = [jnp.exp(p[0] - m) for p in partials]
    acc = sum(p[2] * r for p, r in zip(partials, scales))
    total = sum(p[1] * r for p, r in zip(partials, scales))
    attended = acc / total
    updated = (hidden_in.astype(jnp.float32) + attended).astype(jnp.bfloat16)
    total_conv = stale_all[1]
    totals_conv = total_conv - own_stale[1] + group_moments(updated, GROUPS)
    normed_conv = group_normalize(updated, totals_conv, count, gain_conv, bias_conv, GROUPS)
    activated = jax.nn.silu(normed_conv).astype(jnp.bfloat16).reshape(tok_rows // W, W, channels)
    rows = activated.shape[0]
    count_p = lax.axis_size("patch")
    top = lax.ppermute(
        activated[rows - 1 :], "patch", [(i, i + 1) for i in range(count_p - 1)]
    )
    bottom = lax.ppermute(activated[:1], "patch", [(i + 1, i) for i in range(count_p - 1)])

    def conv_rows(cells):
        return lax.conv_general_dilated(
            cells,
            conv_weight,
            (1, 1),
            ((0, 0), (1, 1)),
            dimension_numbers=("NHWC", "HWIO", "NHWC"),
            preferred_element_type=jnp.float32,
        )

    inner = conv_rows(activated[None])[0]
    edges = conv_rows(
        jnp.stack(
            [
                jnp.concatenate([top, activated[:2]], axis=0),
                jnp.concatenate([activated[rows - 2 :], bottom], axis=0),
            ]
        )
    )
    convolved = jnp.concatenate([edges[0], inner, edges[1]], axis=0)
    temb = time_embedding(timestep, w_time)
    conv_out = (convolved + conv_bias + temb).astype(jnp.bfloat16)
    return conv_out.reshape(tok_rows, conv_weight.shape[3])


def solution(mesh):
    return jax.shard_map(
        body,
        mesh=mesh,
        in_specs=(
            P(("batch", "patch"), None),
            P(("batch", "patch"), None),
            P(("batch", "patch"), None),
            P(("batch", "patch"), None, None, None),
            P(),
            P(),
            P(),
            P(),
            P(),
            P(),
            P(),
            P(),
            P(),
            P(),
            P(),
        ),
        out_specs=P(("batch", "patch"), None),
        check_vma=False,
    )
```
